32 devices in a mesh: region: 8 (over y, x, core), dom: 4 (over z).
Axes of the slice: x: 2, y: 2, z: 4, core: 2. Of those that a mesh axis runs over, the one named last changes fastest.
Arguments:
- feats: bfloat16 [16384, 512], P(('region', 'dom')), may hold values from -6 to 6
- hub_feats: bfloat16 [64, 512], P('region'), may hold values from -6 to 6
- hub_ids: int32 [16384, 4], P(('region', 'dom')), may hold values from 0 to 63
- tile_src: int32 [512], P(('region', 'dom')), may hold values from 0 to 4
- tile_mask: int32 [512, 128, 128], P(('region', 'dom')), may hold values 0 or 1
- w_stack: bfloat16 [1024, 512], replicated, may hold values from -0.1875 to 0.1875
- cotangent: bfloat16 [16384, 512], P(('region', 'dom')), may hold values from -6 to 6
Outputs:
- activ: bfloat16 [16384, 512], P(('region', 'dom'))
- weight_grad: float32 [1024, 512], P('dom')
- hub_grad: float32 [64, 512], P('region')
The draws below stay inside these ranges and needn't reach their ends.
Inputs may be any that keep to these rules, and one draw needn't show every extreme that they name: tile_src names a block of the part's window: 0 is the block taken from the previous part, 1 to 4 are the part's own blocks. `hub_ids`: hub ids index rows of hub_feats.
All inputs are finite; a program needn't handle non-finite values. No bound on the sum of `tile_mask` on one device may be relied on, other than what follows from the above.
Results may differ from the reference program's by a relative error of at most 0.0051.
Values may be sent and summed in bfloat16 or wider, within the bound.
No kernel may reach another device: no remote copies, remote signals or barrier semaphores. Data moves between devices by JAX's collectives and lax.ppermute only.
A program may use at most 64 MiB of HBM per device.

```python
import math
import jax
import jax.numpy as jnp
import numpy as np
from jax import lax

D = 512
TILE = 128
V_DEV = 512
TPB = 4
HUB_K = 4
BLK = 4
TILES = 16
HUBS = 64
NV = 16384
N_REGION = 8
N_DOM = 4
DEVICES = 32


def with_ends(drawn, own_key, smallest, high):
    extent = drawn.shape
    spot = [jax.random.randint(jax.random.fold_in(own_key, axis), (), 0, extent[axis]) for axis in range(len(extent))]
    drawn = drawn.at[tuple(spot)].set(smallest)
    longest = extent.index(max(extent))
    spot[longest] = (spot[longest] + 1) % extent[longest]
    return drawn.at[tuple(spot)].set(high)


def strengthened(result, stream_key, source, target, blocks, factor):
    owner, partner = [(jnp.arange(result.shape[axis_at]) // (result.shape[axis_at] // blocks)).reshape([-1 if axis == axis_at else 1 for axis in range(result.ndim)]) for axis_at in (source, target)]
    chosen = jax.random.permutation(stream_key, blocks)[partner]
    strong = (owner == chosen) | (owner == (partner + blocks // 2) % blocks)
    return jnp.where(strong, factor * result, result)


def block_scale(own_key, dims, split, smallest, largest):
    def one(position, blocks):
        heights = jax.random.uniform(jax.random.fold_in(jax.random.fold_in(own_key, 6), position), (blocks,), jnp.float32, smallest / len(split), largest / len(split))
        return jnp.repeat(jnp.exp(heights), dims[position] // blocks).reshape((-1,) + (1,) * (len(dims) - position - 1))

    level = one(*split[0])
    for cut in split[1:]:
        level = level * one(*cut)
    return level


def cumulative_ranks(amount, lean):
    weights = [(1 << 20) // math.isqrt(grade ** lean) + 1 for grade in range(1, amount + 1)]
    width = 1 + sum(weights) // (1 << 30)
    return np.cumsum(np.array([max(1, weight // width) for weight in weights]))


def ranked(stream_key, shape, count, lean):
    grid = cumulative_ranks(count, lean)
    pick = jax.random.randint(jax.random.fold_in(stream_key, 1), shape, 0, int(grid[count - 1]))
    grade = jnp.searchsorted(jnp.asarray(grid, jnp.int32), pick, side="right")
    return jax.random.permutation(jax.random.fold_in(stream_key, 2), count)[grade].astype(jnp.int32)


def bell_draw(own_key, extent, width, limit, split=(), held_as=jnp.bfloat16):
    array = jax.random.normal(own_key, extent, jnp.float32) * width
    if len(split) > 0:
        array = block_scale(own_key, extent, split, -0.22, 0.18) * array
    return jnp.clip(array, min=-limit, max=limit).astype(held_as)


def heavy_noise(stream_key, shape, width, most, shards, heavy, kind=jnp.bfloat16):
    result = width * jax.random.normal(stream_key, shape, jnp.float32)
    if shards:
        result = result * block_scale(stream_key, shape, shards, -0.22, 0.18)
    return jnp.clip(strengthened(result, jax.random.fold_in(stream_key, 3), *heavy), -most, most).astype(kind)


def setup_inputs(seed: int = 0) -> dict:
    keys = jax.random.split(jax.random.key(seed), 8)
    feats = heavy_noise(keys[0], (NV, D), 1.0, 6.0, ((0, 32),), (0, 1, 32, 2.75))
    hub_feats = bell_draw(keys[1], (HUBS, D), 1.0, 6.0, ((0, 8),))
    hub_ids = with_ends(ranked(keys[2], (NV, HUB_K), HUBS, 2), jax.random.fold_in(keys[2], 3), 0, HUBS - 1).astype(jnp.int32)
    tile_src = with_ends(jax.random.randint(keys[3], (TILES * DEVICES,), 0, BLK + 1), jax.random.fold_in(keys[3], 1), 0, BLK).astype(jnp.int32)
    tile_mask = with_ends((jax.random.randint(keys[4], (TILES * DEVICES, TILE, TILE), 0, 8) < 1).astype(jnp.int32), jax.random.fold_in(keys[4], 1), 0, 1)
    w_stack = bell_draw(keys[5], (2 * D, D), (2 * D) ** -0.5, 0.1875)
    cotangent = bell_draw(keys[6], (NV, D), 1.0, 6.0, ((0, 32),))
    return dict(feats=feats, hub_feats=hub_feats, hub_ids=hub_ids, tile_src=tile_src, tile_mask=tile_mask, w_stack=w_stack, cotangent=cotangent)


def reference(feats, hub_feats, hub_ids, tile_src, tile_mask, w_stack, cotangent):
    parts = N_REGION * N_DOM
    nblk = V_DEV // TILE
    tiles = nblk * TPB
    xs = feats.reshape(parts, V_DEV, D)
    gs = cotangent.reshape(parts, V_DEV, D)
    ids = hub_ids.reshape(parts, V_DEV, HUB_K)
    srcs = tile_src.reshape(parts, tiles)
    masks = tile_mask.reshape(parts, tiles, TILE, TILE)
    lasts = jnp.concatenate([jnp.zeros((1, TILE, D), feats.dtype), xs[:-1, V_DEV - TILE:]], axis=0)
    inside = (jnp.arange(parts) % N_DOM) > 0
    lasts = jnp.where(inside[:, None, None], lasts, jnp.zeros_like(lasts))
    hub_table = hub_feats.astype(jnp.float32)
    w_neigh = w_stack[D:]

    def one_part(carry, item):
        grad_w, grad_h = carry
        x_own, prev, g_own, id_own, src_own, mask_own = item
        window = jnp.concatenate([prev, x_own], axis=0).reshape(nblk + 1, TILE, D)
        picked = window[src_own].astype(jnp.float32)
        mask_f = mask_own.astype(jnp.float32)
        prod = jnp.einsum("tij,tjd->tid", mask_f, picked)
        nsum = prod.reshape(nblk, TPB, TILE, D).sum(axis=1).reshape(V_DEV, D)
        cnt = mask_f.reshape(nblk, TPB, TILE, TILE).sum(axis=(1, 3)).reshape(V_DEV)
        deg = 1.0 + cnt + jnp.float32(HUB_K)
        hsum = hub_table[id_own].sum(axis=1)
        agg = ((x_own.astype(jnp.float32) + nsum + hsum) / deg[:, None]).astype(jnp.bfloat16)
        inputs = jnp.concatenate([x_own, agg], axis=1)
        z = jnp.dot(inputs, w_stack, preferred_element_type=jnp.float32)
        sig = jax.nn.sigmoid(z)
        activ = (z * sig).astype(jnp.bfloat16)
        dz = (g_own.astype(jnp.float32) * sig * (1.0 + z * (1.0 - sig))).astype(jnp.bfloat16)
        grad_w = grad_w + jnp.dot(inputs.T, dz, preferred_element_type=jnp.float32)
        dagg = jnp.dot(dz, w_neigh.T, preferred_element_type=jnp.float32)
        sgrad = (dagg / deg[:, None]).astype(jnp.bfloat16).astype(jnp.float32)
        spread = jnp.broadcast_to(sgrad[:, None, :], (V_DEV, HUB_K, D)).reshape(V_DEV * HUB_K, D)
        grad_h = grad_h + jax.ops.segment_sum(spread, id_own.reshape(V_DEV * HUB_K).astype(jnp.int32), num_segments=HUBS)
        return (grad_w, grad_h), activ

    init = (jnp.zeros((2 * D, D), jnp.float32), jnp.zeros((HUBS, D), jnp.float32))
    (grad_w, grad_h), activ = lax.scan(one_part, init, (xs, lasts, gs, ids, srcs, masks))
    return activ.reshape(parts * V_DEV, D), grad_w, grad_h
```

```python
import jax
import jax.numpy as jnp
from jax import lax
from jax.sharding import PartitionSpec as P


def shifted(value, axis, steps):
    count = lax.axis_size(axis)
    initial, last = (max(0, -steps), min(count, count - steps))
    return lax.ppermute(value, axis, [(source, source + steps) for source in range(initial, last)])


def log2(n):
    bits = n.bit_length() - 1
    assert (1 << bits) == n
    return bits


def swap(value, axis, bit):
    count = lax.axis_size(axis)
    return lax.ppermute(value, axis, [(i, i ^ (1 << bit)) for i in range(count)])


def scatter_sum(value, axis, at, order):
    count = lax.axis_size(axis)
    levels = log2(count)
    me = lax.axis_index(axis)
    shape = value.shape
    value = value.reshape(shape[:at] + (2,) * levels + shape[at + 1 :])
    held = [levels - 1 - k for k in range(levels)]
    for bit in order:
        dim = at + held.index(bit)
        mine = (me >> bit) & 1
        keep = lax.dynamic_index_in_dim(value, mine, axis=dim, keepdims=False)
        send = lax.dynamic_index_in_dim(value, 1 - mine, axis=dim, keepdims=False)
        value = keep + swap(send, axis, bit)
        held.remove(bit)
    return value


def gather_ordered(value, axis, order):
    count = lax.axis_size(axis)
    levels = log2(count)
    me = lax.axis_index(axis)
    rest = value.shape
    held = []
    for bit in order:
        other = swap(value, axis, bit)
        mine = ((me >> bit) & 1) == 0
        low = jnp.where(mine, value, other)
        high = jnp.where(mine, other, value)
        value = jnp.stack([low, high], axis=0)
        held.insert(0, bit)
    natural = [held.index(levels - 1 - k) for k in range(levels)]
    value = jnp.transpose(value, natural + list(range(levels, levels + len(rest))))
    return value.reshape((count,) + rest)


def sum_all(value, axis):
    for bit in range(log2(lax.axis_size(axis))):
        value = value + swap(value, axis, bit)
    return value


def on_device(feats, hub_feats, hub_ids, tile_src, tile_mask, w_stack, cotangent):
    rows, width = feats.shape
    tile = tile_mask.shape[1]
    nblk = rows // tile
    per_block = tile_src.shape[0] // nblk
    hub_count = hub_ids.shape[1]
    owned = hub_feats.shape[0]
    regions = lax.axis_size("region")
    doms = lax.axis_size("dom")
    total_hubs = owned * regions
    up = list(range(log2(regions)))
    down = up[::-1]
    prev = shifted(feats[rows - tile :], "dom", 1)
    hub_table = gather_ordered(hub_feats, "region", down).reshape(total_hubs, width)
    window = jnp.concatenate([prev, feats], axis=0).reshape(nblk + 1, tile, width)
    picked = jnp.take(window, tile_src, axis=0)
    mask_b = tile_mask.astype(jnp.bfloat16)
    prod = jnp.einsum("tij,tjd->tid", mask_b, picked, preferred_element_type=jnp.float32)
    nsum = prod.reshape(nblk, per_block, tile, width).sum(axis=1).reshape(rows, width)
    cnt = tile_mask.reshape(nblk, per_block, tile, tile).sum(axis=(1, 3)).reshape(rows)
    deg = 1.0 + cnt.astype(jnp.float32) + jnp.float32(hub_count)
    hub_cols = lax.broadcasted_iota(jnp.int32, (rows, total_hubs), 1)
    counts = jnp.zeros((rows, total_hubs), jnp.float32)
    for slot in range(hub_count):
        counts = counts + (hub_ids[:, slot : slot + 1] == hub_cols).astype(jnp.float32)
    counts = counts.astype(jnp.bfloat16)
    hsum = jnp.dot(counts, hub_table, preferred_element_type=jnp.float32)
    agg = ((feats.astype(jnp.float32) + nsum + hsum) / deg[:, None]).astype(jnp.bfloat16)
    inputs = jnp.concatenate([feats, agg], axis=1)
    z = jnp.dot(inputs, w_stack, preferred_element_type=jnp.float32)
    sig = jax.nn.sigmoid(z)
    activ = (z * sig).astype(jnp.bfloat16)
    dz = (cotangent.astype(jnp.float32) * sig * (1.0 + z * (1.0 - sig))).astype(jnp.bfloat16)
    partial_w = lax.dot_general(inputs, dz, (((0,), (0,)), ((), ())), preferred_element_type=jnp.float32)
    span = partial_w.shape[0] // (doms * regions)
    partial_w = partial_w.reshape(doms, regions, span, width)
    region_w = scatter_sum(partial_w, "region", 1, up)
    piece_w = scatter_sum(region_w, "dom", 0, list(range(log2(doms))))
    weight_grad = gather_ordered(piece_w, "region", down).reshape(regions * span, width)
    dagg = lax.dot_general(
        dz, w_stack[width:], (((1,), (1,)), ((), ())), preferred_element_type=jnp.float32
    )
    sgrad = (dagg / deg[:, None]).astype(jnp.bfloat16)
    partial_h = lax.dot_general(counts, sgrad, (((0,), (0,)), ((), ())), preferred_element_type=jnp.float32)
    partial_h = partial_h.reshape(regions, owned, width)
    hub_grad = sum_all(scatter_sum(partial_h, "region", 0, up), "dom")
    return (activ, weight_grad, hub_grad)


def solution(mesh):
    placed = (
        P(("region", "dom"), None),
        P("region", None),
        P(("region", "dom"), None),
        P(("region", "dom")),
        P(("region", "dom"), None, None),
        P(),
        P(("region", "dom"), None),
    )
    return jax.shard_map(
        on_device,
        mesh=mesh,
        in_specs=placed,
        out_specs=(P(("region", "dom"), None), P("dom", None), P("region", None)),
        check_vma=False,
    )
```

```python
import jax
import jax.numpy as jnp
from jax import lax
from jax.sharding import PartitionSpec as P


def shifted(value, axis, steps):
    count = lax.axis_size(axis)
    initial, last = (max(0, -steps), min(count, count - steps))
    return lax.ppermute(value, axis, [(source, source + steps) for source in range(initial, last)])


def log2(n):
    bits = n.bit_length() - 1
    assert (1 << bits) == n
    return bits


def swap(value, axis, bit):
    count = lax.axis_size(axis)
    return lax.ppermute(value, axis, [(i, i ^ (1 << bit)) for i in range(count)])


def scatter_sum(value, axis, at, order, other=None):
    count = lax.axis_size(axis)
    levels = log2(count)
    me = lax.axis_index(axis)
    other = order if other is None else other
    first = (me & 1) == 0
    shape = value.shape
    value = value.reshape(shape[:at] + (2,) * levels + shape[at + 1 :])
    held = [[levels - 1 - k for k in range(levels)] for _ in range(2)]
    for bit, bit_b in zip(order, other):
        parts = []
        for group, b in enumerate((bit, bit_b)):
            dim = at + held[group].index(b)
            mine = (me >> b) & 1
            keep = lax.dynamic_index_in_dim(value, mine, axis=dim, keepdims=False)
            send = lax.dynamic_index_in_dim(value, 1 - mine, axis=dim, keepdims=False)
            parts.append((keep, send))
            held[group].remove(b)
        if bit == bit_b:
            keep, send = parts[0]
            value = keep + swap(send, axis, bit)
        else:
            keep = jnp.where(first, parts[0][0], parts[1][0])
            send = jnp.where(first, parts[0][1], parts[1][1])
            pairs = [(i, i ^ (1 << (bit if i & 1 == 0 else bit_b))) for i in range(count)]
            value = keep + lax.ppermute(send, axis, pairs)
    assert held[0] == held[1] or levels == 0
    return value


def gather_small(value, axis):
    count = lax.axis_size(axis)
    spread = jnp.broadcast_to(value[None], (count,) + value.shape)
    return lax.all_to_all(spread, axis, 0, 0)


def gather_ordered(value, axis, order):
    count = lax.axis_size(axis)
    levels = log2(count)
    me = lax.axis_index(axis)
    rest = value.shape
    held = []
    for bit in order:
        other = swap(value, axis, bit)
        mine = ((me >> bit) & 1) == 0
        low = jnp.where(mine, value, other)
        high = jnp.where(mine, other, value)
        value = jnp.stack([low, high], axis=0)
        held.insert(0, bit)
    natural = [held.index(levels - 1 - k) for k in range(levels)]
    value = jnp.transpose(value, natural + list(range(levels, levels + len(rest))))
    return value.reshape((count,) + rest)


def sum_all(value, axis):
    for bit in range(log2(lax.axis_size(axis))):
        value = value + swap(value, axis, bit)
    return value


def on_device(feats, hub_feats, hub_ids, tile_src, tile_mask, w_stack, cotangent):
    rows, width = feats.shape
    tile = tile_mask.shape[1]
    nblk = rows // tile
    per_block = tile_src.shape[0] // nblk
    hub_count = hub_ids.shape[1]
    owned = hub_feats.shape[0]
    regions = lax.axis_size("region")
    doms = lax.axis_size("dom")
    total_hubs = owned * regions
    up = list(range(log2(regions)))
    down = up[::-1]
    prev = shifted(feats[rows - tile :], "dom", 1)
    hub_table = gather_small(hub_feats, "region").reshape(total_hubs, width)
    window = jnp.concatenate([prev, feats], axis=0).reshape(nblk + 1, tile, width)
    picked = jnp.take(window, tile_src, axis=0)
    mask_b = tile_mask.astype(jnp.bfloat16)
    prod = jnp.einsum("tij,tjd->tid", mask_b, picked, preferred_element_type=jnp.float32)
    nsum = prod.reshape(nblk, per_block, tile, width).sum(axis=1).reshape(rows, width)
    cnt = tile_mask.reshape(nblk, per_block, tile, tile).sum(axis=(1, 3)).reshape(rows)
    deg = 1.0 + cnt.astype(jnp.float32) + jnp.float32(hub_count)
    hub_cols = lax.broadcasted_iota(jnp.int32, (rows, total_hubs), 1)
    counts = jnp.zeros((rows, total_hubs), jnp.float32)
    for slot in range(hub_count):
        counts = counts + (hub_ids[:, slot : slot + 1] == hub_cols).astype(jnp.float32)
    counts = counts.astype(jnp.bfloat16)
    hsum = jnp.dot(counts, hub_table, preferred_element_type=jnp.float32)
    agg = ((feats.astype(jnp.float32) + nsum + hsum) / deg[:, None]).astype(jnp.bfloat16)
    inputs = jnp.concatenate([feats, agg], axis=1)
    z = jnp.dot(inputs, w_stack, preferred_element_type=jnp.float32)
    sig = jax.nn.sigmoid(z)
    activ = (z * sig).astype(jnp.bfloat16)
    dz = (cotangent.astype(jnp.float32) * sig * (1.0 + z * (1.0 - sig))).astype(jnp.bfloat16)
    partial_w = lax.dot_general(inputs, dz, (((0,), (0,)), ((), ())), preferred_element_type=jnp.float32)
    span = partial_w.shape[0] // (doms * regions)
    partial_w = partial_w.reshape(doms, regions, span, width)
    region_w = scatter_sum(partial_w, "region", 1, up, up[:1] + up[1:][::-1])
    piece_w = scatter_sum(region_w, "dom", 0, list(range(log2(doms))))
    weight_grad = gather_ordered(piece_w, "region", down).reshape(regions * span, width)
    dagg = lax.dot_general(
        dz, w_stack[width:], (((1,), (1,)), ((), ())), preferred_element_type=jnp.float32
    )
    sgrad = (dagg / deg[:, None]).astype(jnp.bfloat16)
    partial_h = lax.dot_general(counts, sgrad, (((0,), (0,)), ((), ())), preferred_element_type=jnp.float32)
    partial_h = partial_h.reshape(regions, owned, width)
    region_h = lax.all_to_all(partial_h, "region", 0, 0).sum(axis=0)
    hub_grad = gather_small(region_h, "dom").sum(axis=0)
    return (activ, weight_grad, hub_grad)


def solution(mesh):
    placed = (
        P(("region", "dom"), None),
        P("region", None),
        P(("region", "dom"), None),
        P(("region", "dom")),
        P(("region", "dom"), None, None),
        P(),
        P(("region", "dom"), None),
    )
    return jax.shard_map(
        on_device,
        mesh=mesh,
        in_specs=placed,
        out_specs=(P(("region", "dom"), None), P("dom", None), P("region", None)),
        check_vma=False,
    )
```

```python
import jax
import jax.numpy as jnp
from jax import lax
from jax.sharding import PartitionSpec as P


def shifted(value, axis, steps):
    count = lax.axis_size(axis)
    initial, last = (max(0, -steps), min(count, count - steps))
    return lax.ppermute(value, axis, [(source, source + steps) for source in range(initial, last)])


def log2(n):
    bits = n.bit_length() - 1
    assert (1 << bits) == n
    return bits


def swap(value, axis, bit):
    count = lax.axis_size(axis)
    return lax.ppermute(value, axis, [(i, i ^ (1 << bit)) for i in range(count)])


def scatter_sum(value, axis, at, order, other=None):
    count = lax.axis_size(axis)
    levels = log2(count)
    me = lax.axis_index(axis)
    other = order if other is None else other
    first = (me & 1) == 0
    shape = value.shape
    value = value.reshape(shape[:at] + (2,) * levels + shape[at + 1 :])
    held = [[levels - 1 - k for k in range(levels)] for _ in range(2)]
    for bit, bit_b in zip(order, other):
        parts = []
        for group, b in enumerate((bit, bit_b)):
            dim = at + held[group].index(b)
            mine = (me >> b) & 1
            keep = lax.dynamic_index_in_dim(value, mine, axis=dim, keepdims=False)
            send = lax.dynamic_index_in_dim(value, 1 - mine, axis=dim, keepdims=False)
            parts.append((keep, send))
            held[group].remove(b)
        if bit == bit_b:
            keep, send = parts[0]
            value = keep + swap(send, axis, bit)
        else:
            keep = jnp.where(first, parts[0][0], parts[1][0])
            send = jnp.where(first, parts[0][1], parts[1][1])
            pairs = [(i, i ^ (1 << (bit if i & 1 == 0 else bit_b))) for i in range(count)]
            value = keep + lax.ppermute(send, axis, pairs)
    assert held[0] == held[1] or levels == 0
    return value


def gather_ordered(value, axis, order):
    count = lax.axis_size(axis)
    levels = log2(count)
    me = lax.axis_index(axis)
    rest = value.shape
    held = []
    for bit in order:
        other = swap(value, axis, bit)
        mine = ((me >> bit) & 1) == 0
        low = jnp.where(mine, value, other)
        high = jnp.where(mine, other, value)
        value = jnp.stack([low, high], axis=0)
        held.insert(0, bit)
    natural = [held.index(levels - 1 - k) for k in range(levels)]
    value = jnp.transpose(value, natural + list(range(levels, levels + len(rest))))
    return value.reshape((count,) + rest)


def sum_all(value, axis):
    for bit in range(log2(lax.axis_size(axis))):
        value = value + swap(value, axis, bit)
    return value


def on_device(feats, hub_feats, hub_ids, tile_src, tile_mask, w_stack, cotangent):
    rows, width = feats.shape
    tile = tile_mask.shape[1]
    nblk = rows // tile
    per_block = tile_src.shape[0] // nblk
    hub_count = hub_ids.shape[1]
    owned = hub_feats.shape[0]
    regions = lax.axis_size("region")
    doms = lax.axis_size("dom")
    total_hubs = owned * regions
    up = list(range(log2(regions)))
    down = up[::-1]
    prev = shifted(feats[rows - tile :], "dom", 1)
    hub_table = gather_ordered(hub_feats, "region", down).reshape(total_hubs, width)
    window = jnp.concatenate([prev, feats], axis=0)
    src = tile_src.reshape(nblk, per_block)
    chosen = src[:, :, None] == lax.broadcasted_iota(jnp.int32, (nblk, per_block, nblk + 1), 2)
    masks = tile_mask.reshape(nblk, per_block, tile, 1, tile)
    links = jnp.where(chosen[:, :, None, :, None], masks, 0).sum(axis=1)
    links = links.reshape(rows, (nblk + 1) * tile)
    nsum = jnp.dot(links.astype(jnp.bfloat16), window, preferred_element_type=jnp.float32)
    cnt = tile_mask.reshape(nblk, per_block, tile, tile).sum(axis=(1, 3)).reshape(rows)
    deg = 1.0 + cnt.astype(jnp.float32) + jnp.float32(hub_count)
    hub_cols = lax.broadcasted_iota(jnp.int32, (rows, total_hubs), 1)
    counts = jnp.zeros((rows, total_hubs), jnp.float32)
    for slot in range(hub_count):
        counts = counts + (hub_ids[:, slot : slot + 1] == hub_cols).astype(jnp.float32)
    counts = counts.astype(jnp.bfloat16)
    hsum = jnp.dot(counts, hub_table, preferred_element_type=jnp.float32)
    agg = ((feats.astype(jnp.float32) + nsum + hsum) / deg[:, None]).astype(jnp.bfloat16)
    inputs = jnp.concatenate([feats, agg], axis=1)
    z = jnp.dot(inputs, w_stack, preferred_element_type=jnp.float32)
    sig = jax.nn.sigmoid(z)
    activ = (z * sig).astype(jnp.bfloat16)
    dz = (cotangent.astype(jnp.float32) * sig * (1.0 + z * (1.0 - sig))).astype(jnp.bfloat16)
    partial_w = lax.dot_general(inputs, dz, (((0,), (0,)), ((), ())), preferred_element_type=jnp.float32)
    span = partial_w.shape[0] // (doms * regions)
    partial_w = partial_w.reshape(doms, regions, span, width)
    region_w = scatter_sum(partial_w, "region", 1, up, up[:1] + up[1:][::-1])
    piece_w = scatter_sum(region_w, "dom", 0, list(range(log2(doms))))
    weight_grad = gather_ordered(piece_w, "region", down).reshape(regions * span, width)
    dagg = lax.dot_general(
        dz, w_stack[width:], (((1,), (1,)), ((), ())), preferred_element_type=jnp.float32
    )
    sgrad = (dagg / deg[:, None]).astype(jnp.bfloat16)
    partial_h = lax.dot_general(counts, sgrad, (((0,), (0,)), ((), ())), preferred_element_type=jnp.float32)
    partial_h = partial_h.reshape(regions, owned, width)
    hub_grad = sum_all(scatter_sum(partial_h, "region", 0, up), "dom")
    return (activ, weight_grad, hub_grad)


def solution(mesh):
    placed = (
        P(("region", "dom"), None),
        P("region", None),
        P(("region", "dom"), None),
        P(("region", "dom")),
        P(("region", "dom"), None, None),
        P(),
        P(("region", "dom"), None),
    )
    return jax.shard_map(
        on_device,
        mesh=mesh,
        in_specs=placed,
        out_specs=(P(("region", "dom"), None), P("dom", None), P("region", None)),
        check_vma=False,
    )
```

```python
import jax
import jax.numpy as jnp
from jax import lax
from jax.sharding import PartitionSpec as P


def shifted(value, axis, steps):
    count = lax.axis_size(axis)
    initial, last = (max(0, -steps), min(count, count - steps))
    return lax.ppermute(value, axis, [(source, source + steps) for source in range(initial, last)])


def log2(n):
    bits = n.bit_length() - 1
    assert (1 << bits) == n
    return bits


def swap(value, axis, bit):
    count = lax.axis_size(axis)
    return lax.ppermute(value, axis, [(i, i ^ (1 << bit)) for i in range(count)])


def scatter_sum(value, axis, at, order, other=None, after_first=None):
    count = lax.axis_size(axis)
    levels = log2(count)
    me = lax.axis_index(axis)
    other = order if other is None else other
    first = (me & 1) == 0
    shape = value.shape
    value = value.reshape(shape[:at] + (2,) * levels + shape[at + 1 :])
    held = [[levels - 1 - k for k in range(levels)] for _ in range(2)]
    for bit, bit_b in zip(order, other):
        parts = []
        for group, b in enumerate((bit, bit_b)):
            dim = at + held[group].index(b)
            mine = (me >> b) & 1
            keep = lax.dynamic_index_in_dim(value, mine, axis=dim, keepdims=False)
            send = lax.dynamic_index_in_dim(value, 1 - mine, axis=dim, keepdims=False)
            parts.append((keep, send))
            held[group].remove(b)
        if bit == bit_b:
            keep, send = parts[0]
            value = keep + swap(send, axis, bit)
        else:
            keep = jnp.where(first, parts[0][0], parts[1][0])
            send = jnp.where(first, parts[0][1], parts[1][1])
            pairs = [(i, i ^ (1 << (bit if i & 1 == 0 else bit_b))) for i in range(count)]
            value = keep + lax.ppermute(send, axis, pairs)
        if after_first is not None:
            value = after_first(value)
            after_first = None
    assert held[0] == held[1] or levels == 0
    return value


def gather_ordered(value, axis, order):
    count = lax.axis_size(axis)
    levels = log2(count)
    me = lax.axis_index(axis)
    rest = value.shape
    held = []
    for bit in order:
        other = swap(value, axis, bit)
        mine = ((me >> bit) & 1) == 0
        low = jnp.where(mine, value, other)
        high = jnp.where(mine, other, value)
        value = jnp.stack([low, high], axis=0)
        held.insert(0, bit)
    natural = [held.index(levels - 1 - k) for k in range(levels)]
    value = jnp.transpose(value, natural + list(range(levels, levels + len(rest))))
    return value.reshape((count,) + rest)


def gather_once(value, axis):
    count = lax.axis_size(axis)
    me = lax.axis_index(axis)
    got = [value] + [swap_by(value, axis, k) for k in range(1, count)]
    got = jnp.stack(got, axis=0)
    return jnp.take(got, me ^ lax.broadcasted_iota(jnp.int32, (count,), 0), axis=0)


def swap_by(value, axis, mask):
    count = lax.axis_size(axis)
    return lax.ppermute(value, axis, [(i, i ^ mask) for i in range(count)])


def sum_all(value, axis):
    for bit in range(log2(lax.axis_size(axis))):
        value = value + swap(value, axis, bit)
    return value


def on_device(feats, hub_feats, hub_ids, tile_src, tile_mask, w_stack, cotangent):
    rows, width = feats.shape
    tile = tile_mask.shape[1]
    nblk = rows // tile
    per_block = tile_src.shape[0] // nblk
    hub_count = hub_ids.shape[1]
    owned = hub_feats.shape[0]
    regions = lax.axis_size("region")
    doms = lax.axis_size("dom")
    total_hubs = owned * regions
    up = list(range(log2(regions)))
    down = up[::-1]
    prev = shifted(feats[rows - tile :], "dom", 1)
    hub_table = gather_once(hub_feats, "region").reshape(total_hubs, width)
    window = jnp.concatenate([prev, feats], axis=0)
    src = tile_src.reshape(nblk, per_block)
    chosen = src[:, :, None] == lax.broadcasted_iota(jnp.int32, (nblk, per_block, nblk + 1), 2)
    masks = tile_mask.reshape(nblk, per_block, tile, 1, tile)
    links = jnp.where(chosen[:, :, None, :, None], masks, 0).sum(axis=1)
    links = links.reshape(rows, (nblk + 1) * tile)
    nsum = jnp.dot(links.astype(jnp.bfloat16), window, preferred_element_type=jnp.float32)
    cnt = tile_mask.reshape(nblk, per_block, tile, tile).sum(axis=(1, 3)).reshape(rows)
    deg = 1.0 + cnt.astype(jnp.float32) + jnp.float32(hub_count)
    hub_cols = lax.broadcasted_iota(jnp.int32, (rows, total_hubs), 1)
    counts = jnp.zeros((rows, total_hubs), jnp.float32)
    for slot in range(hub_count):
        counts = counts + (hub_ids[:, slot : slot + 1] == hub_cols).astype(jnp.float32)
    counts = counts.astype(jnp.bfloat16)
    hsum = jnp.dot(counts, hub_table, preferred_element_type=jnp.float32)
    agg = ((feats.astype(jnp.float32) + nsum + hsum) / deg[:, None]).astype(jnp.bfloat16)
    inputs = jnp.concatenate([feats, agg], axis=1)
    z = jnp.dot(inputs, w_stack, preferred_element_type=jnp.float32)
    sig = jax.nn.sigmoid(z)
    activ = (z * sig).astype(jnp.bfloat16)
    dz = (cotangent.astype(jnp.float32) * sig * (1.0 + z * (1.0 - sig))).astype(jnp.bfloat16)
    partial_w = lax.dot_general(inputs, dz, (((0,), (0,)), ((), ())), preferred_element_type=jnp.float32)
    span = partial_w.shape[0] // (doms * regions)
    partial_w = partial_w.reshape(doms, regions, span, width)
    dagg = lax.dot_general(
        dz, w_stack[width:], (((1,), (1,)), ((), ())), preferred_element_type=jnp.float32
    )
    sgrad = (dagg / deg[:, None]).astype(jnp.bfloat16)
    partial_h = lax.dot_general(counts, sgrad, (((0,), (0,)), ((), ())), preferred_element_type=jnp.float32)
    partial_h = partial_h.reshape(regions, owned, width)
    held = {}

    def hub_first(value):
        value, held["h"] = lax.optimization_barrier((value, partial_h))
        return value

    region_w = scatter_sum(partial_w, "region", 1, up, up[:1] + up[1:][::-1], hub_first)
    hub_grad = sum_all(scatter_sum(held["h"], "region", 0, up), "dom")
    piece_w = scatter_sum(region_w, "dom", 0, list(range(log2(doms))))
    weight_grad = gather_ordered(piece_w, "region", down).reshape(regions * span, width)
    return (activ, weight_grad, hub_grad)


def solution(mesh):
    placed = (
        P(("region", "dom"), None),
        P("region", None),
        P(("region", "dom"), None),
        P(("region", "dom")),
        P(("region", "dom"), None, None),
        P(),
        P(("region", "dom"), None),
    )
    return jax.shard_map(
        on_device,
        mesh=mesh,
        in_specs=placed,
        out_specs=(P(("region", "dom"), None), P("dom", None), P("region", None)),
        check_vma=False,
    )
```

```python
import jax
import jax.numpy as jnp
from jax import lax
from jax.sharding import PartitionSpec as P


def shifted(value, axis, steps):
    count = lax.axis_size(axis)
    initial, last = (max(0, -steps), min(count, count - steps))
    return lax.ppermute(value, axis, [(source, source + steps) for source in range(initial, last)])


def log2(n):
    bits = n.bit_length() - 1
    assert (1 << bits) == n
    return bits


def swap(value, axis, bit):
    count = lax.axis_size(axis)
    return lax.ppermute(value, axis, [(i, i ^ (1 << bit)) for i in range(count)])


def exchange(sends, axis, pairs):
    width = sends[0].shape[-1]
    flat = jnp.concatenate([x.reshape(-1, width) for x in sends], axis=0)
    flat = lax.ppermute(flat, axis, pairs)
    got, start = [], 0
    for x in sends:
        size = x.size // width
        got.append(flat[start : start + size].reshape(x.shape))
        start += size
    return got


def scatter_sum(values, axis, ats, order, other=None, riders=()):
    count = lax.axis_size(axis)
    levels = log2(count)
    me = lax.axis_index(axis)
    other = order if other is None else other
    first = (me & 1) == 0
    values = [
        v.reshape(v.shape[:at] + (2,) * levels + v.shape[at + 1 :]) for v, at in zip(values, ats)
    ]
    riders = list(riders)
    held = [[levels - 1 - k for k in range(levels)] for _ in range(2)]
    for bit, bit_b in zip(order, other):
        dims = []
        for group, b in enumerate((bit, bit_b)):
            dims.append(held[group].index(b))
            held[group].remove(b)
        keeps, sends = [], []
        for v, at in zip(values, ats):
            parts = []
            for b, dim in zip((bit, bit_b), dims):
                mine = (me >> b) & 1
                keep = lax.dynamic_index_in_dim(v, mine, axis=at + dim, keepdims=False)
                send = lax.dynamic_index_in_dim(v, 1 - mine, axis=at + dim, keepdims=False)
                parts.append((keep, send))
            if bit == bit_b:
                keeps.append(parts[0][0])
                sends.append(parts[0][1])
            else:
                keeps.append(jnp.where(first, parts[0][0], parts[1][0]))
                sends.append(jnp.where(first, parts[0][1], parts[1][1]))
        pairs = [(i, i ^ (1 << (bit if i & 1 == 0 else bit_b))) for i in range(count)]
        got = exchange(sends + riders, axis, pairs)
        values = [k + g for k, g in zip(keeps, got)]
        riders = [r + g for r, g in zip(riders, got[len(keeps) :])]
    return values, riders


def gather_ordered(value, axis, order):
    count = lax.axis_size(axis)
    levels = log2(count)
    me = lax.axis_index(axis)
    rest = value.shape
    held = []
    for bit in order:
        other = swap(value, axis, bit)
        mine = ((me >> bit) & 1) == 0
        low = jnp.where(mine, value, other)
        high = jnp.where(mine, other, value)
        value = jnp.stack([low, high], axis=0)
        held.insert(0, bit)
    natural = [held.index(levels - 1 - k) for k in range(levels)]
    value = jnp.transpose(value, natural + list(range(levels, levels + len(rest))))
    return value.reshape((count,) + rest)


def on_device(feats, hub_feats, hub_ids, tile_src, tile_mask, w_stack, cotangent):
    rows, width = feats.shape
    tile = tile_mask.shape[1]
    nblk = rows // tile
    per_block = tile_src.shape[0] // nblk
    hub_count = hub_ids.shape[1]
    owned = hub_feats.shape[0]
    regions = lax.axis_size("region")
    doms = lax.axis_size("dom")
    total_hubs = owned * regions
    up = list(range(log2(regions)))
    down = up[::-1]
    prev = shifted(feats[rows - tile :], "dom", 1)
    hub_table = gather_ordered(hub_feats, "region", down).reshape(total_hubs, width)
    window = jnp.concatenate([prev, feats], axis=0)
    src = tile_src.reshape(nblk, per_block)
    chosen = src[:, :, None] == lax.broadcasted_iota(jnp.int32, (nblk, per_block, nblk + 1), 2)
    masks = tile_mask.reshape(nblk, per_block, tile, 1, tile)
    links = jnp.where(chosen[:, :, None, :, None], masks, 0).sum(axis=1)
    links = links.reshape(rows, (nblk + 1) * tile)
    nsum = jnp.dot(links.astype(jnp.bfloat16), window, preferred_element_type=jnp.float32)
    cnt = tile_mask.reshape(nblk, per_block, tile, tile).sum(axis=(1, 3)).reshape(rows)
    deg = 1.0 + cnt.astype(jnp.float32) + jnp.float32(hub_count)
    hub_cols = lax.broadcasted_iota(jnp.int32, (rows, total_hubs), 1)
    counts = jnp.zeros((rows, total_hubs), jnp.float32)
    for slot in range(hub_count):
        counts = counts + (hub_ids[:, slot : slot + 1] == hub_cols).astype(jnp.float32)
    counts = counts.astype(jnp.bfloat16)
    hsum = jnp.dot(counts, hub_table, preferred_element_type=jnp.float32)
    agg = ((feats.astype(jnp.float32) + nsum + hsum) / deg[:, None]).astype(jnp.bfloat16)
    inputs = jnp.concatenate([feats, agg], axis=1)
    z = jnp.dot(inputs, w_stack, preferred_element_type=jnp.float32)
    sig = jax.nn.sigmoid(z)
    activ = (z * sig).astype(jnp.bfloat16)
    dz = (cotangent.astype(jnp.float32) * sig * (1.0 + z * (1.0 - sig))).astype(jnp.bfloat16)
    partial_w = lax.dot_general(inputs, dz, (((0,), (0,)), ((), ())), preferred_element_type=jnp.float32)
    span = partial_w.shape[0] // (doms * regions)
    partial_w = partial_w.reshape(doms, regions, span, width)
    dagg = lax.dot_general(
        dz, w_stack[width:], (((1,), (1,)), ((), ())), preferred_element_type=jnp.float32
    )
    sgrad = (dagg / deg[:, None]).astype(jnp.bfloat16)
    partial_h = lax.dot_general(counts, sgrad, (((0,), (0,)), ((), ())), preferred_element_type=jnp.float32)
    partial_h = partial_h.reshape(regions, owned, width)
    (region_w, region_h), _ = scatter_sum(
        [partial_w, partial_h], "region", [1, 0], up, up[:1] + up[1:][::-1]
    )
    (piece_w,), (hub_grad,) = scatter_sum(
        [region_w], "dom", [0], list(range(log2(doms))), riders=[region_h]
    )
    weight_grad = gather_ordered(piece_w, "region", down).reshape(regions * span, width)
    return (activ, weight_grad, hub_grad)


def solution(mesh):
    placed = (
        P(("region", "dom"), None),
        P("region", None),
        P(("region", "dom"), None),
        P(("region", "dom")),
        P(("region", "dom"), None, None),
        P(),
        P(("region", "dom"), None),
    )
    return jax.shard_map(
        on_device,
        mesh=mesh,
        in_specs=placed,
        out_specs=(P(("region", "dom"), None), P("dom", None), P("region", None)),
        check_vma=False,
    )
```

```python
import jax
import jax.numpy as jnp
from jax import lax
from jax.sharding import PartitionSpec as P


def shifted(value, axis, steps):
    count = lax.axis_size(axis)
    initial, last = (max(0, -steps), min(count, count - steps))
    return lax.ppermute(value, axis, [(source, source + steps) for source in range(initial, last)])


def log2(n):
    bits = n.bit_length() - 1
    assert (1 << bits) == n
    return bits


def swap(value, axis, bit):
    count = lax.axis_size(axis)
    return lax.ppermute(value, axis, [(i, i ^ (1 << bit)) for i in range(count)])


def exchange(sends, axis, pairs):
    width = sends[0].shape[-1]
    flat = jnp.concatenate([x.reshape(-1, width) for x in sends], axis=0)
    flat = lax.ppermute(flat, axis, pairs)
    got, start = [], 0
    for x in sends:
        size = x.size // width
        got.append(flat[start : start + size].reshape(x.shape))
        start += size
    return got


def scatter_sum(values, axis, ats, order, other=None, riders=(), joins=None):
    count = lax.axis_size(axis)
    levels = log2(count)
    me = lax.axis_index(axis)
    other = order if other is None else other
    joins = [0] * len(values) if joins is None else joins
    first = (me & 1) == 0
    values = [
        v.reshape(v.shape[:at] + (2,) * levels + v.shape[at + 1 :]) for v, at in zip(values, ats)
    ]
    riders = list(riders)
    held = [[[levels - 1 - k for k in range(levels)] for _ in range(2)] for _ in values]
    for step, (bit, bit_b) in enumerate(zip(order, other)):
        active = [i for i in range(len(values)) if joins[i] <= step]
        keeps, sends = [], []
        for i in active:
            v, at = values[i], ats[i]
            parts = []
            for group, b in enumerate((bit, bit_b)):
                dim = at + held[i][group].index(b)
                held[i][group].remove(b)
                mine = (me >> b) & 1
                keep = lax.dynamic_index_in_dim(v, mine, axis=dim, keepdims=False)
                send = lax.dynamic_index_in_dim(v, 1 - mine, axis=dim, keepdims=False)
                parts.append((keep, send))
            if bit == bit_b:
                keeps.append(parts[0][0])
                sends.append(parts[0][1])
            else:
                keeps.append(jnp.where(first, parts[0][0], parts[1][0]))
                sends.append(jnp.where(first, parts[0][1], parts[1][1]))
        pairs = [(i, i ^ (1 << (bit if i & 1 == 0 else bit_b))) for i in range(count)]
        got = exchange(sends + riders, axis, pairs)
        for i, k, g in zip(active, keeps, got):
            values[i] = k + g
        riders = [r + g for r, g in zip(riders, got[len(keeps) :])]
    return values, riders


def gather_ordered(value, axis, order, rider=None):
    count = lax.axis_size(axis)
    levels = log2(count)
    me = lax.axis_index(axis)
    rest = value.shape
    held = []
    for bit in order:
        mine = (me >> bit) & 1
        if rider is not None and bit == 0:
            keep = lax.dynamic_index_in_dim(rider, mine, axis=0, keepdims=False)
            send = lax.dynamic_index_in_dim(rider, 1 - mine, axis=0, keepdims=False)
            other, got = exchange([value, send], axis, [(i, i ^ 1) for i in range(count)])
            rider = keep + got
        else:
            other = swap(value, axis, bit)
        low = jnp.where(mine == 0, value, other)
        high = jnp.where(mine == 0, other, value)
        value = jnp.stack([low, high], axis=0)
        held.insert(0, bit)
    natural = [held.index(levels - 1 - k) for k in range(levels)]
    value = jnp.transpose(value, natural + list(range(levels, levels + len(rest))))
    return value.reshape((count,) + rest), rider


def on_device(feats, hub_feats, hub_ids, tile_src, tile_mask, w_stack, cotangent):
    rows, width = feats.shape
    tile = tile_mask.shape[1]
    nblk = rows // tile
    per_block = tile_src.shape[0] // nblk
    hub_count = hub_ids.shape[1]
    owned = hub_feats.shape[0]
    regions = lax.axis_size("region")
    doms = lax.axis_size("dom")
    total_hubs = owned * regions
    up = list(range(log2(regions)))
    down = up[::-1]
    prev = shifted(feats[rows - tile :], "dom", 1)
    hub_table = gather_ordered(hub_feats, "region", down)[0].reshape(total_hubs, width)
    window = jnp.concatenate([prev, feats], axis=0)
    src = tile_src.reshape(nblk, per_block)
    chosen = src[:, :, None] == lax.broadcasted_iota(jnp.int32, (nblk, per_block, nblk + 1), 2)
    masks = tile_mask.reshape(nblk, per_block, tile, 1, tile)
    links = jnp.where(chosen[:, :, None, :, None], masks, 0).sum(axis=1)
    links = links.reshape(rows, (nblk + 1) * tile)
    nsum = jnp.dot(links.astype(jnp.bfloat16), window, preferred_element_type=jnp.float32)
    cnt = tile_mask.reshape(nblk, per_block, tile, tile).sum(axis=(1, 3)).reshape(rows)
    deg = 1.0 + cnt.astype(jnp.float32) + jnp.float32(hub_count)
    hub_cols = lax.broadcasted_iota(jnp.int32, (rows, total_hubs), 1)
    counts = jnp.zeros((rows, total_hubs), jnp.float32)
    for slot in range(hub_count):
        counts = counts + (hub_ids[:, slot : slot + 1] == hub_cols).astype(jnp.float32)
    counts = counts.astype(jnp.bfloat16)
    hsum = jnp.dot(counts, hub_table, preferred_element_type=jnp.float32)
    agg = ((feats.astype(jnp.float32) + nsum + hsum) / deg[:, None]).astype(jnp.bfloat16)
    inputs = jnp.concatenate([feats, agg], axis=1)
    z = jnp.dot(inputs, w_stack, preferred_element_type=jnp.float32)
    sig = jax.nn.sigmoid(z)
    activ = (z * sig).astype(jnp.bfloat16)
    dz = (cotangent.astype(jnp.float32) * sig * (1.0 + z * (1.0 - sig))).astype(jnp.bfloat16)
    partial_w = lax.dot_general(inputs, dz, (((0,), (0,)), ((), ())), preferred_element_type=jnp.float32)
    span = partial_w.shape[0] // (doms * regions)
    partial_w = partial_w.reshape(doms, regions, span, width)
    dagg = lax.dot_general(
        dz, w_stack[width:], (((1,), (1,)), ((), ())), preferred_element_type=jnp.float32
    )
    sgrad = (dagg / deg[:, None]).astype(jnp.bfloat16)
    partial_h = lax.dot_general(counts, sgrad, (((0,), (0,)), ((), ())), preferred_element_type=jnp.float32)
    partial_h = partial_h.reshape(regions, owned, width)
    (region_w, region_h), _ = scatter_sum(
        [partial_w, partial_h], "region", [1, 0], up, up[:1] + up[1:][::-1], joins=[0, 1]
    )
    (piece_w,), (region_h,) = scatter_sum(
        [region_w], "dom", [0], list(range(log2(doms))), riders=[region_h]
    )
    weight_grad, hub_grad = gather_ordered(piece_w, "region", down, region_h)
    weight_grad = weight_grad.reshape(regions * span, width)
    return (activ, weight_grad, hub_grad)


def solution(mesh):
    placed = (
        P(("region", "dom"), None),
        P("region", None),
        P(("region", "dom"), None),
        P(("region", "dom")),
        P(("region", "dom"), None, None),
        P(),
        P(("region", "dom"), None),
    )
    return jax.shard_map(
        on_device,
        mesh=mesh,
        in_specs=placed,
        out_specs=(P(("region", "dom"), None), P("dom", None), P("region", None)),
        check_vma=False,
    )
```

```python
import jax
import jax.numpy as jnp
from jax import lax
from jax.sharding import PartitionSpec as P


def shifted(value, axis, steps):
    count = lax.axis_size(axis)
    initial, last = (max(0, -steps), min(count, count - steps))
    return lax.ppermute(value, axis, [(source, source + steps) for source in range(initial, last)])


def log2(n):
    bits = n.bit_length() - 1
    assert (1 << bits) == n
    return bits


def swap(value, axis, bit):
    count = lax.axis_size(axis)
    return lax.ppermute(value, axis, [(i, i ^ (1 << bit)) for i in range(count)])


def exchange(sends, axis, pairs, wire=None):
    width = sends[0].shape[-1]
    flat = jnp.concatenate([x.reshape(-1, width) for x in sends], axis=0)
    kind = flat.dtype
    flat = flat if wire is None else flat.astype(wire)
    flat = lax.ppermute(flat, axis, pairs).astype(kind)
    got, start = [], 0
    for x in sends:
        size = x.size // width
        got.append(flat[start : start + size].reshape(x.shape))
        start += size
    return got


def scatter_sum(values, axis, ats, order, other=None, riders=(), joins=None, wires=None):
    count = lax.axis_size(axis)
    levels = log2(count)
    me = lax.axis_index(axis)
    other = order if other is None else other
    joins = [0] * len(values) if joins is None else joins
    first = (me & 1) == 0
    values = [
        v.reshape(v.shape[:at] + (2,) * levels + v.shape[at + 1 :]) for v, at in zip(values, ats)
    ]
    riders = list(riders)
    held = [[[levels - 1 - k for k in range(levels)] for _ in range(2)] for _ in values]
    for step, (bit, bit_b) in enumerate(zip(order, other)):
        active = [i for i in range(len(values)) if joins[i] <= step]
        keeps, sends = [], []
        for i in active:
            v, at = values[i], ats[i]
            parts = []
            for group, b in enumerate((bit, bit_b)):
                dim = at + held[i][group].index(b)
                held[i][group].remove(b)
                mine = (me >> b) & 1
                keep = lax.dynamic_index_in_dim(v, mine, axis=dim, keepdims=False)
                send = lax.dynamic_index_in_dim(v, 1 - mine, axis=dim, keepdims=False)
                parts.append((keep, send))
            if bit == bit_b:
                keeps.append(parts[0][0])
                sends.append(parts[0][1])
            else:
                keeps.append(jnp.where(first, parts[0][0], parts[1][0]))
                sends.append(jnp.where(first, parts[0][1], parts[1][1]))
        pairs = [(i, i ^ (1 << (bit if i & 1 == 0 else bit_b))) for i in range(count)]
        got = exchange(sends + riders, axis, pairs, None if wires is None else wires[step])
        for i, k, g in zip(active, keeps, got):
            values[i] = k + g
        riders = [r + g for r, g in zip(riders, got[len(keeps) :])]
    return values, riders


def gather_ordered(value, axis, order, rider=None, other=None):
    count = lax.axis_size(axis)
    levels = log2(count)
    me = lax.axis_index(axis)
    other = order if other is None else other
    first = (me & 1) == 0
    rest = value.shape
    held = [[], []]
    for bit, bit_b in zip(order, other):
        if bit == bit_b and held[0] != held[1]:
            swapped = [held[1].index(b) for b in held[0]]
            tail = list(range(len(swapped), value.ndim))
            value = jnp.where(first, value, jnp.transpose(value, swapped + tail))
            held[1] = list(held[0])
        pairs = [(i, i ^ (1 << (bit if i & 1 == 0 else bit_b))) for i in range(count)]
        if rider is not None and bit == 0:
            mine = me & 1
            keep = lax.dynamic_index_in_dim(rider, mine, axis=0, keepdims=False)
            send = lax.dynamic_index_in_dim(rider, 1 - mine, axis=0, keepdims=False)
            got, got_rider = exchange([value, send], axis, pairs)
            rider = keep + got_rider
        else:
            got = lax.ppermute(value, axis, pairs)
        mine = jnp.where(first, (me >> bit) & 1, (me >> bit_b) & 1)
        low = jnp.where(mine == 0, value, got)
        high = jnp.where(mine == 0, got, value)
        value = jnp.stack([low, high], axis=0)
        held[0].insert(0, bit)
        held[1].insert(0, bit_b)
    tail = list(range(levels, levels + len(rest)))
    ways = []
    for group in range(2):
        natural = [held[group].index(levels - 1 - k) for k in range(levels)]
        ways.append(jnp.transpose(value, natural + tail).reshape((count,) + rest))
    value = ways[0] if held[0] == held[1] else jnp.where(first, ways[0], ways[1])
    return value, rider


def on_device(feats, hub_feats, hub_ids, tile_src, tile_mask, w_stack, cotangent):
    rows, width = feats.shape
    tile = tile_mask.shape[1]
    nblk = rows // tile
    per_block = tile_src.shape[0] // nblk
    hub_count = hub_ids.shape[1]
    owned = hub_feats.shape[0]
    regions = lax.axis_size("region")
    doms = lax.axis_size("dom")
    total_hubs = owned * regions
    up = list(range(log2(regions)))
    down = up[::-1]
    prev = shifted(feats[rows - tile :], "dom", 1)
    hub_table = gather_ordered(hub_feats, "region", down)[0].reshape(total_hubs, width)
    window = jnp.concatenate([prev, feats], axis=0)
    src = tile_src.reshape(nblk, per_block)
    chosen = src[:, :, None] == lax.broadcasted_iota(jnp.int32, (nblk, per_block, nblk + 1), 2)
    masks = tile_mask.reshape(nblk, per_block, tile, 1, tile)
    links = jnp.where(chosen[:, :, None, :, None], masks, 0).sum(axis=1)
    links = links.reshape(rows, (nblk + 1) * tile)
    nsum = jnp.dot(links.astype(jnp.bfloat16), window, preferred_element_type=jnp.float32)
    cnt = tile_mask.reshape(nblk, per_block, tile, tile).sum(axis=(1, 3)).reshape(rows)
    deg = 1.0 + cnt.astype(jnp.float32) + jnp.float32(hub_count)
    hub_cols = lax.broadcasted_iota(jnp.int32, (rows, total_hubs), 1)
    counts = jnp.zeros((rows, total_hubs), jnp.float32)
    for slot in range(hub_count):
        counts = counts + (hub_ids[:, slot : slot + 1] == hub_cols).astype(jnp.float32)
    counts = counts.astype(jnp.bfloat16)
    hsum = jnp.dot(counts, hub_table, preferred_element_type=jnp.float32)
    agg = ((feats.astype(jnp.float32) + nsum + hsum) / deg[:, None]).astype(jnp.bfloat16)
    inputs = jnp.concatenate([feats, agg], axis=1)
    z = jnp.dot(inputs, w_stack, preferred_element_type=jnp.float32)
    sig = jax.nn.sigmoid(z)
    activ = (z * sig).astype(jnp.bfloat16)
    dz = (cotangent.astype(jnp.float32) * sig * (1.0 + z * (1.0 - sig))).astype(jnp.bfloat16)
    partial_w = lax.dot_general(inputs, dz, (((0,), (0,)), ((), ())), preferred_element_type=jnp.float32)
    span = partial_w.shape[0] // (doms * regions)
    partial_w = partial_w.reshape(doms, regions, span, width)
    dagg = lax.dot_general(
        dz, w_stack[width:], (((1,), (1,)), ((), ())), preferred_element_type=jnp.float32
    )
    sgrad = (dagg / deg[:, None]).astype(jnp.bfloat16)
    partial_h = lax.dot_general(counts, sgrad, (((0,), (0,)), ((), ())), preferred_element_type=jnp.float32)
    partial_h = partial_h.reshape(regions, owned, width)
    (region_w, region_h), _ = scatter_sum(
        [partial_w, partial_h], "region", [1, 0], up, up[:1] + up[1:][::-1], joins=[0, 1],
        wires=None,
    )
    (piece_w,), (region_h,) = scatter_sum(
        [region_w], "dom", [0], list(range(log2(doms))), riders=[region_h],
        wires=None,
    )
    weight_grad, hub_grad = gather_ordered(
        piece_w, "region", down, region_h, down[:-1][::-1] + down[-1:]
    )
    weight_grad = weight_grad.reshape(regions * span, width)
    return (activ, weight_grad, hub_grad)


def solution(mesh):
    placed = (
        P(("region", "dom"), None),
        P("region", None),
        P(("region", "dom"), None),
        P(("region", "dom")),
        P(("region", "dom"), None, None),
        P(),
        P(("region", "dom"), None),
    )
    return jax.shard_map(
        on_device,
        mesh=mesh,
        in_specs=placed,
        out_specs=(P(("region", "dom"), None), P("dom", None), P("region", None)),
        check_vma=False,
    )
```

```python
import jax
import jax.numpy as jnp
from jax import lax
from jax.sharding import PartitionSpec as P


def shifted(value, axis, steps):
    count = lax.axis_size(axis)
    initial, last = (max(0, -steps), min(count, count - steps))
    return lax.ppermute(value, axis, [(source, source + steps) for source in range(initial, last)])


def log2(n):
    bits = n.bit_length() - 1
    assert (1 << bits) == n
    return bits


def swap(value, axis, bit):
    count = lax.axis_size(axis)
    return lax.ppermute(value, axis, [(i, i ^ (1 << bit)) for i in range(count)])


def exchange(sends, axis, pairs, wire=None):
    width = sends[0].shape[-1]
    flat = jnp.concatenate([x.reshape(-1, width) for x in sends], axis=0)
    kind = flat.dtype
    flat = flat if wire is None else flat.astype(wire)
    flat = lax.ppermute(flat, axis, pairs).astype(kind)
    got, start = [], 0
    for x in sends:
        size = x.size // width
        got.append(flat[start : start + size].reshape(x.shape))
        start += size
    return got


def scatter_sum(values, axis, ats, order, other=None, riders=(), joins=None, wires=None):
    count = lax.axis_size(axis)
    levels = log2(count)
    me = lax.axis_index(axis)
    other = order if other is None else other
    joins = [0] * len(values) if joins is None else joins
    first = (me & 1) == 0
    values = [
        v.reshape(v.shape[:at] + (2,) * levels + v.shape[at + 1 :]) for v, at in zip(values, ats)
    ]
    riders = list(riders)
    held = [[[levels - 1 - k for k in range(levels)] for _ in range(2)] for _ in values]
    for step, (bit, bit_b) in enumerate(zip(order, other)):
        active = [i for i in range(len(values)) if joins[i] <= step]
        keeps, sends = [], []
        for i in active:
            v, at = values[i], ats[i]
            parts = []
            for group, b in enumerate((bit, bit_b)):
                dim = at + held[i][group].index(b)
                held[i][group].remove(b)
                mine = (me >> b) & 1
                keep = lax.dynamic_index_in_dim(v, mine, axis=dim, keepdims=False)
                send = lax.dynamic_index_in_dim(v, 1 - mine, axis=dim, keepdims=False)
                parts.append((keep, send))
            if bit == bit_b:
                keeps.append(parts[0][0])
                sends.append(parts[0][1])
            else:
                keeps.append(jnp.where(first, parts[0][0], parts[1][0]))
                sends.append(jnp.where(first, parts[0][1], parts[1][1]))
        pairs = [(i, i ^ (1 << (bit if i & 1 == 0 else bit_b))) for i in range(count)]
        got = exchange(sends + riders, axis, pairs, None if wires is None else wires[step])
        for i, k, g in zip(active, keeps, got):
            values[i] = k + g
        riders = [r + g for r, g in zip(riders, got[len(keeps) :])]
    return values, riders


def gather_ordered(value, axis, order, rider=None, other=None, hook=None):
    count = lax.axis_size(axis)
    levels = log2(count)
    me = lax.axis_index(axis)
    other = order if other is None else other
    first = (me & 1) == 0
    rest = value.shape
    held = [[], []]
    for bit, bit_b in zip(order, other):
        if bit == bit_b and held[0] != held[1]:
            swapped = [held[1].index(b) for b in held[0]]
            tail = list(range(len(swapped), value.ndim))
            value = jnp.where(first, value, jnp.transpose(value, swapped + tail))
            held[1] = list(held[0])
        pairs = [(i, i ^ (1 << (bit if i & 1 == 0 else bit_b))) for i in range(count)]
        if rider is not None and bit == 0:
            mine = me & 1
            keep = lax.dynamic_index_in_dim(rider, mine, axis=0, keepdims=False)
            send = lax.dynamic_index_in_dim(rider, 1 - mine, axis=0, keepdims=False)
            got, got_rider = exchange([value, send], axis, pairs)
            rider = keep + got_rider
        else:
            got = lax.ppermute(value, axis, pairs)
        mine = jnp.where(first, (me >> bit) & 1, (me >> bit_b) & 1)
        low = jnp.where(mine == 0, value, got)
        high = jnp.where(mine == 0, got, value)
        value = jnp.stack([low, high], axis=0)
        if hook is not None:
            value = hook(value)
            hook = None
        held[0].insert(0, bit)
        held[1].insert(0, bit_b)
    tail = list(range(levels, levels + len(rest)))
    ways = []
    for group in range(2):
        natural = [held[group].index(levels - 1 - k) for k in range(levels)]
        ways.append(jnp.transpose(value, natural + tail).reshape((count,) + rest))
    value = ways[0] if held[0] == held[1] else jnp.where(first, ways[0], ways[1])
    return value, rider


def on_device(feats, hub_feats, hub_ids, tile_src, tile_mask, w_stack, cotangent):
    rows, width = feats.shape
    tile = tile_mask.shape[1]
    nblk = rows // tile
    per_block = tile_src.shape[0] // nblk
    hub_count = hub_ids.shape[1]
    owned = hub_feats.shape[0]
    regions = lax.axis_size("region")
    doms = lax.axis_size("dom")
    total_hubs = owned * regions
    up = list(range(log2(regions)))
    down = up[::-1]
    prev = shifted(feats[rows - tile :], "dom", 1)
    held = {}

    def mask_after(value):
        value, held["mask"] = lax.optimization_barrier((value, tile_mask))
        return value

    hub_table = gather_ordered(hub_feats, "region", down, hook=mask_after)[0]
    hub_table = hub_table.reshape(total_hubs, width)
    tile_mask = held["mask"]
    window = jnp.concatenate([prev, feats], axis=0)
    src = tile_src.reshape(nblk, per_block)
    chosen = src[:, :, None] == lax.broadcasted_iota(jnp.int32, (nblk, per_block, nblk + 1), 2)
    masks = tile_mask.reshape(nblk, per_block, tile, 1, tile)
    links = jnp.where(chosen[:, :, None, :, None], masks, 0).sum(axis=1)
    links = links.reshape(rows, (nblk + 1) * tile)
    nsum = jnp.dot(links.astype(jnp.bfloat16), window, preferred_element_type=jnp.float32)
    cnt = tile_mask.reshape(nblk, per_block, tile, tile).sum(axis=(1, 3)).reshape(rows)
    deg = 1.0 + cnt.astype(jnp.float32) + jnp.float32(hub_count)
    hub_cols = lax.broadcasted_iota(jnp.int32, (rows, total_hubs), 1)
    counts = jnp.zeros((rows, total_hubs), jnp.float32)
    for slot in range(hub_count):
        counts = counts + (hub_ids[:, slot : slot + 1] == hub_cols).astype(jnp.float32)
    counts = counts.astype(jnp.bfloat16)
    hsum = jnp.dot(counts, hub_table, preferred_element_type=jnp.float32)
    agg = ((feats.astype(jnp.float32) + nsum + hsum) / deg[:, None]).astype(jnp.bfloat16)
    inputs = jnp.concatenate([feats, agg], axis=1)
    z = jnp.dot(inputs, w_stack, preferred_element_type=jnp.float32)
    sig = jax.nn.sigmoid(z)
    activ = (z * sig).astype(jnp.bfloat16)
    dz = (cotangent.astype(jnp.float32) * sig * (1.0 + z * (1.0 - sig))).astype(jnp.bfloat16)
    partial_w = lax.dot_general(inputs, dz, (((0,), (0,)), ((), ())), preferred_element_type=jnp.float32)
    span = partial_w.shape[0] // (doms * regions)
    partial_w = partial_w.reshape(doms, regions, span, width)
    dagg = lax.dot_general(
        dz, w_stack[width:], (((1,), (1,)), ((), ())), preferred_element_type=jnp.float32
    )
    sgrad = (dagg / deg[:, None]).astype(jnp.bfloat16)
    partial_h = lax.dot_general(counts, sgrad, (((0,), (0,)), ((), ())), preferred_element_type=jnp.float32)
    partial_h = partial_h.reshape(regions, owned, width)
    (region_w, region_h), _ = scatter_sum(
        [partial_w, partial_h], "region", [1, 0], up, up[:1] + up[1:][::-1], joins=[0, 1],
        wires=None,
    )
    (piece_w,), (region_h,) = scatter_sum(
        [region_w], "dom", [0], list(range(log2(doms))), riders=[region_h],
        wires=None,
    )
    weight_grad, hub_grad = gather_ordered(
        piece_w, "region", down, region_h, down[:-1][::-1] + down[-1:]
    )
    weight_grad = weight_grad.reshape(regions * span, width)
    return (activ, weight_grad, hub_grad)


def solution(mesh):
    placed = (
        P(("region", "dom"), None),
        P("region", None),
        P(("region", "dom"), None),
        P(("region", "dom")),
        P(("region", "dom"), None, None),
        P(),
        P(("region", "dom"), None),
    )
    return jax.shard_map(
        on_device,
        mesh=mesh,
        in_specs=placed,
        out_specs=(P(("region", "dom"), None), P("dom", None), P("region", None)),
        check_vma=False,
    )
```

```python
import jax
import jax.numpy as jnp
from jax import lax
from jax.sharding import PartitionSpec as P


def shifted(value, axis, steps):
    count = lax.axis_size(axis)
    initial, last = (max(0, -steps), min(count, count - steps))
    return lax.ppermute(value, axis, [(source, source + steps) for source in range(initial, last)])


def log2(n):
    bits = n.bit_length() - 1
    assert (1 << bits) == n
    return bits


def swap(value, axis, bit):
    count = lax.axis_size(axis)
    return lax.ppermute(value, axis, [(i, i ^ (1 << bit)) for i in range(count)])


def exchange(sends, axis, pairs, wire=None):
    width = sends[0].shape[-1]
    flat = jnp.concatenate([x.reshape(-1, width) for x in sends], axis=0)
    kind = flat.dtype
    flat = flat if wire is None else flat.astype(wire)
    flat = lax.ppermute(flat, axis, pairs).astype(kind)
    got, start = [], 0
    for x in sends:
        size = x.size // width
        got.append(flat[start : start + size].reshape(x.shape))
        start += size
    return got


def scatter_sum(values, axis, ats, order, other=None, riders=(), joins=None, wires=None):
    count = lax.axis_size(axis)
    levels = log2(count)
    me = lax.axis_index(axis)
    other = order if other is None else other
    joins = [0] * len(values) if joins is None else joins
    first = (me & 1) == 0
    values = [
        v.reshape(v.shape[:at] + (2,) * levels + v.shape[at + 1 :]) for v, at in zip(values, ats)
    ]
    riders = list(riders)
    held = [[[levels - 1 - k for k in range(levels)] for _ in range(2)] for _ in values]
    for step, (bit, bit_b) in enumerate(zip(order, other)):
        active = [i for i in range(len(values)) if joins[i] <= step]
        keeps, sends = [], []
        for i in active:
            v, at = values[i], ats[i]
            parts = []
            for group, b in enumerate((bit, bit_b)):
                dim = at + held[i][group].index(b)
                held[i][group].remove(b)
                mine = (me >> b) & 1
                keep = lax.dynamic_index_in_dim(v, mine, axis=dim, keepdims=False)
                send = lax.dynamic_index_in_dim(v, 1 - mine, axis=dim, keepdims=False)
                parts.append((keep, send))
            if bit == bit_b:
                keeps.append(parts[0][0])
                sends.append(parts[0][1])
            else:
                keeps.append(jnp.where(first, parts[0][0], parts[1][0]))
                sends.append(jnp.where(first, parts[0][1], parts[1][1]))
        pairs = [(i, i ^ (1 << (bit if i & 1 == 0 else bit_b))) for i in range(count)]
        got = exchange(sends + riders, axis, pairs, None if wires is None else wires[step])
        for i, k, g in zip(active, keeps, got):
            values[i] = k + g
        riders = [r + g for r, g in zip(riders, got[len(keeps) :])]
    return values, riders


def gather_ordered(value, axis, order, rider=None, other=None):
    count = lax.axis_size(axis)
    levels = log2(count)
    me = lax.axis_index(axis)
    other = order if other is None else other
    first = (me & 1) == 0
    rest = value.shape
    held = [[], []]
    for bit, bit_b in zip(order, other):
        if bit == bit_b and held[0] != held[1]:
            swapped = [held[1].index(b) for b in held[0]]
            tail = list(range(len(swapped), value.ndim))
            value = jnp.where(first, value, jnp.transpose(value, swapped + tail))
            held[1] = list(held[0])
        pairs = [(i, i ^ (1 << (bit if i & 1 == 0 else bit_b))) for i in range(count)]
        if rider is not None and bit == 0:
            mine = me & 1
            keep = lax.dynamic_index_in_dim(rider, mine, axis=0, keepdims=False)
            send = lax.dynamic_index_in_dim(rider, 1 - mine, axis=0, keepdims=False)
            got, got_rider = exchange([value, send], axis, pairs)
            rider = keep + got_rider
        else:
            got = lax.ppermute(value, axis, pairs)
        mine = jnp.where(first, (me >> bit) & 1, (me >> bit_b) & 1)
        low = jnp.where(mine == 0, value, got)
        high = jnp.where(mine == 0, got, value)
        value = jnp.stack([low, high], axis=0)
        held[0].insert(0, bit)
        held[1].insert(0, bit_b)
    tail = list(range(levels, levels + len(rest)))
    ways = []
    for group in range(2):
        natural = [held[group].index(levels - 1 - k) for k in range(levels)]
        ways.append(jnp.transpose(value, natural + tail).reshape((count,) + rest))
    value = ways[0] if held[0] == held[1] else jnp.where(first, ways[0], ways[1])
    return value, rider


def scatter_once(value, axis, riders):
    count = lax.axis_size(axis)
    me = lax.axis_index(axis)
    total = lax.dynamic_index_in_dim(value, me, axis=0, keepdims=False)
    seen = [[r] for r in riders]
    for k in range(1, count):
        pairs = [(i, i ^ k) for i in range(count)]
        send = lax.dynamic_index_in_dim(value, me ^ k, axis=0, keepdims=False)
        got = exchange([send] + list(riders), axis, pairs)
        total = total + got[0]
        for r, g in zip(seen, got[1:]):
            r.append(g)
    order = me ^ lax.broadcasted_iota(jnp.int32, (count,), 0)
    riders = [jnp.take(jnp.stack(r, axis=0), order, axis=0).sum(axis=0) for r in seen]
    return total, riders


def gather_once(value, axis, rider=None):
    count = lax.axis_size(axis)
    me = lax.axis_index(axis)
    got = [value]
    for k in range(1, count):
        pairs = [(i, i ^ k) for i in range(count)]
        if rider is not None and k == 1:
            mine = me & 1
            keep = lax.dynamic_index_in_dim(rider, mine, axis=0, keepdims=False)
            send = lax.dynamic_index_in_dim(rider, 1 - mine, axis=0, keepdims=False)
            g, g_rider = exchange([value, send], axis, pairs)
            rider = keep + g_rider
        else:
            g = lax.ppermute(value, axis, pairs)
        got.append(g)
    order = me ^ lax.broadcasted_iota(jnp.int32, (count,), 0)
    return jnp.take(jnp.stack(got, axis=0), order, axis=0), rider


def on_device(feats, hub_feats, hub_ids, tile_src, tile_mask, w_stack, cotangent):
    rows, width = feats.shape
    tile = tile_mask.shape[1]
    nblk = rows // tile
    per_block = tile_src.shape[0] // nblk
    hub_count = hub_ids.shape[1]
    owned = hub_feats.shape[0]
    regions = lax.axis_size("region")
    doms = lax.axis_size("dom")
    total_hubs = owned * regions
    up = list(range(log2(regions)))
    down = up[::-1]
    prev = shifted(feats[rows - tile :], "dom", 1)
    hub_table = gather_ordered(hub_feats, "region", down)[0].reshape(total_hubs, width)
    window = jnp.concatenate([prev, feats], axis=0)
    src = tile_src.reshape(nblk, per_block)
    chosen = src[:, :, None] == lax.broadcasted_iota(jnp.int32, (nblk, per_block, nblk + 1), 2)
    masks = tile_mask.reshape(nblk, per_block, tile, 1, tile)
    links = jnp.where(chosen[:, :, None, :, None], masks, 0).sum(axis=1)
    links = links.reshape(rows, (nblk + 1) * tile)
    nsum = jnp.dot(links.astype(jnp.bfloat16), window, preferred_element_type=jnp.float32)
    cnt = tile_mask.reshape(nblk, per_block, tile, tile).sum(axis=(1, 3)).reshape(rows)
    deg = 1.0 + cnt.astype(jnp.float32) + jnp.float32(hub_count)
    hub_cols = lax.broadcasted_iota(jnp.int32, (rows, total_hubs), 1)
    counts = jnp.zeros((rows, total_hubs), jnp.float32)
    for slot in range(hub_count):
        counts = counts + (hub_ids[:, slot : slot + 1] == hub_cols).astype(jnp.float32)
    counts = counts.astype(jnp.bfloat16)
    hsum = jnp.dot(counts, hub_table, preferred_element_type=jnp.float32)
    agg = ((feats.astype(jnp.float32) + nsum + hsum) / deg[:, None]).astype(jnp.bfloat16)
    inputs = jnp.concatenate([feats, agg], axis=1)
    z = jnp.dot(inputs, w_stack, preferred_element_type=jnp.float32)
    sig = jax.nn.sigmoid(z)
    activ = (z * sig).astype(jnp.bfloat16)
    dz = (cotangent.astype(jnp.float32) * sig * (1.0 + z * (1.0 - sig))).astype(jnp.bfloat16)
    partial_w = lax.dot_general(inputs, dz, (((0,), (0,)), ((), ())), preferred_element_type=jnp.float32)
    span = partial_w.shape[0] // (doms * regions)
    partial_w = partial_w.reshape(doms, regions, span, width)
    dagg = lax.dot_general(
        dz, w_stack[width:], (((1,), (1,)), ((), ())), preferred_element_type=jnp.float32
    )
    sgrad = (dagg / deg[:, None]).astype(jnp.bfloat16)
    partial_h = lax.dot_general(counts, sgrad, (((0,), (0,)), ((), ())), preferred_element_type=jnp.float32)
    partial_h = partial_h.reshape(regions, owned, width)
    (region_w, region_h), _ = scatter_sum(
        [partial_w, partial_h], "region", [1, 0], up, up[:1] + up[1:][::-1], joins=[0, 1],
        wires=None,
    )
    if doms <= 8:
        piece_w, (region_h,) = scatter_once(region_w, "dom", [region_h])
    else:
        (piece_w,), (region_h,) = scatter_sum(
            [region_w], "dom", [0], list(range(log2(doms))), riders=[region_h]
        )
    if regions <= 8:
        weight_grad, hub_grad = gather_once(piece_w, "region", region_h)
    else:
        weight_grad, hub_grad = gather_ordered(
            piece_w, "region", down, region_h, down[:-1][::-1] + down[-1:]
        )
    weight_grad = weight_grad.reshape(regions * span, width)
    return (activ, weight_grad, hub_grad)


def solution(mesh):
    placed = (
        P(("region", "dom"), None),
        P("region", None),
        P(("region", "dom"), None),
        P(("region", "dom")),
        P(("region", "dom"), None, None),
        P(),
        P(("region", "dom"), None),
    )
    return jax.shard_map(
        on_device,
        mesh=mesh,
        in_specs=placed,
        out_specs=(P(("region", "dom"), None), P("dom", None), P("region", None)),
        check_vma=False,
    )
```

```python
import jax
import jax.numpy as jnp
from jax import lax
from jax.sharding import PartitionSpec as P


def shifted(value, axis, steps):
    count = lax.axis_size(axis)
    initial, last = (max(0, -steps), min(count, count - steps))
    return lax.ppermute(value, axis, [(source, source + steps) for source in range(initial, last)])


def log2(n):
    bits = n.bit_length() - 1
    assert (1 << bits) == n
    return bits


def swap(value, axis, bit):
    count = lax.axis_size(axis)
    return lax.ppermute(value, axis, [(i, i ^ (1 << bit)) for i in range(count)])


def exchange(sends, axis, pairs, wire=None):
    width = sends[0].shape[-1]
    flat = jnp.concatenate([x.reshape(-1, width) for x in sends], axis=0)
    kind = flat.dtype
    flat = flat if wire is None else flat.astype(wire)
    flat = lax.ppermute(flat, axis, pairs).astype(kind)
    got, start = [], 0
    for x in sends:
        size = x.size // width
        got.append(flat[start : start + size].reshape(x.shape))
        start += size
    return got


def scatter_sum(values, axis, ats, order, other=None, riders=(), joins=None, wires=None):
    count = lax.axis_size(axis)
    levels = log2(count)
    me = lax.axis_index(axis)
    other = order if other is None else other
    joins = [0] * len(values) if joins is None else joins
    first = (me & 1) == 0
    values = [
        v.reshape(v.shape[:at] + (2,) * levels + v.shape[at + 1 :]) for v, at in zip(values, ats)
    ]
    riders = list(riders)
    held = [[[levels - 1 - k for k in range(levels)] for _ in range(2)] for _ in values]
    for step, (bit, bit_b) in enumerate(zip(order, other)):
        active = [i for i in range(len(values)) if joins[i] <= step]
        keeps, sends = [], []
        for i in active:
            v, at = values[i], ats[i]
            parts = []
            for group, b in enumerate((bit, bit_b)):
                dim = at + held[i][group].index(b)
                held[i][group].remove(b)
                mine = (me >> b) & 1
                keep = lax.dynamic_index_in_dim(v, mine, axis=dim, keepdims=False)
                send = lax.dynamic_index_in_dim(v, 1 - mine, axis=dim, keepdims=False)
                parts.append((keep, send))
            if bit == bit_b:
                keeps.append(parts[0][0])
                sends.append(parts[0][1])
            else:
                keeps.append(jnp.where(first, parts[0][0], parts[1][0]))
                sends.append(jnp.where(first, parts[0][1], parts[1][1]))
        pairs = [(i, i ^ (1 << (bit if i & 1 == 0 else bit_b))) for i in range(count)]
        got = exchange(sends + riders, axis, pairs, None if wires is None else wires[step])
        for i, k, g in zip(active, keeps, got):
            values[i] = k + g
        riders = [r + g for r, g in zip(riders, got[len(keeps) :])]
    return values, riders


def gather_ordered(value, axis, order, rider=None, other=None):
    count = lax.axis_size(axis)
    levels = log2(count)
    me = lax.axis_index(axis)
    other = order if other is None else other
    first = (me & 1) == 0
    rest = value.shape
    held = [[], []]
    for bit, bit_b in zip(order, other):
        if bit == bit_b and held[0] != held[1]:
            swapped = [held[1].index(b) for b in held[0]]
            tail = list(range(len(swapped), value.ndim))
            value = jnp.where(first, value, jnp.transpose(value, swapped + tail))
            held[1] = list(held[0])
        pairs = [(i, i ^ (1 << (bit if i & 1 == 0 else bit_b))) for i in range(count)]
        if rider is not None and bit == 0:
            mine = me & 1
            keep = lax.dynamic_index_in_dim(rider, mine, axis=0, keepdims=False)
            send = lax.dynamic_index_in_dim(rider, 1 - mine, axis=0, keepdims=False)
            got, got_rider = exchange([value, send], axis, pairs)
            rider = keep + got_rider
        else:
            got = lax.ppermute(value, axis, pairs)
        mine = jnp.where(first, (me >> bit) & 1, (me >> bit_b) & 1)
        low = jnp.where(mine == 0, value, got)
        high = jnp.where(mine == 0, got, value)
        value = jnp.stack([low, high], axis=0)
        held[0].insert(0, bit)
        held[1].insert(0, bit_b)
    tail = list(range(levels, levels + len(rest)))
    ways = []
    for group in range(2):
        natural = [held[group].index(levels - 1 - k) for k in range(levels)]
        ways.append(jnp.transpose(value, natural + tail).reshape((count,) + rest))
    value = ways[0] if held[0] == held[1] else jnp.where(first, ways[0], ways[1])
    return value, rider


def on_device(feats, hub_feats, hub_ids, tile_src, tile_mask, w_stack, cotangent):
    rows, width = feats.shape
    tile = tile_mask.shape[1]
    nblk = rows // tile
    per_block = tile_src.shape[0] // nblk
    hub_count = hub_ids.shape[1]
    owned = hub_feats.shape[0]
    regions = lax.axis_size("region")
    doms = lax.axis_size("dom")
    total_hubs = owned * regions
    up = list(range(log2(regions)))
    down = up[::-1]
    prev = shifted(feats[rows - tile :], "dom", 1)
    hub_table = gather_ordered(hub_feats, "region", down)[0].reshape(total_hubs, width)
    window = jnp.concatenate([prev, feats], axis=0)
    src = tile_src.reshape(nblk, per_block)
    chosen = src[:, :, None] == lax.broadcasted_iota(jnp.int32, (nblk, per_block, nblk + 1), 2)
    masks = tile_mask.reshape(nblk, per_block, tile, 1, tile)
    links = jnp.where(chosen[:, :, None, :, None], masks, 0).sum(axis=1)
    links = links.reshape(rows, (nblk + 1) * tile)
    nsum = jnp.dot(links.astype(jnp.bfloat16), window, preferred_element_type=jnp.float32)
    cnt = tile_mask.reshape(nblk, per_block, tile, tile).sum(axis=(1, 3)).reshape(rows)
    deg = 1.0 + cnt.astype(jnp.float32) + jnp.float32(hub_count)
    hub_cols = lax.broadcasted_iota(jnp.int32, (rows, total_hubs), 1)
    counts = jnp.zeros((rows, total_hubs), jnp.float32)
    for slot in range(hub_count):
        counts = counts + (hub_ids[:, slot : slot + 1] == hub_cols).astype(jnp.float32)
    counts = counts.astype(jnp.bfloat16)
    hsum = jnp.dot(counts, hub_table, preferred_element_type=jnp.float32)
    agg = ((feats.astype(jnp.float32) + nsum + hsum) / deg[:, None]).astype(jnp.bfloat16)
    inputs = jnp.concatenate([feats, agg], axis=1)
    z = jnp.dot(inputs, w_stack, preferred_element_type=jnp.float32)
    sig = jax.nn.sigmoid(z)
    activ = (z * sig).astype(jnp.bfloat16)
    dz = (cotangent.astype(jnp.float32) * sig * (1.0 + z * (1.0 - sig))).astype(jnp.bfloat16)
    partial_w = lax.dot_general(inputs, dz, (((0,), (0,)), ((), ())), preferred_element_type=jnp.float32)
    span = partial_w.shape[0] // (doms * regions)
    partial_w = partial_w.reshape(doms, regions, span, width)
    dagg = lax.dot_general(
        dz, w_stack[width:], (((1,), (1,)), ((), ())), preferred_element_type=jnp.float32
    )
    sgrad = (dagg / deg[:, None]).astype(jnp.bfloat16)
    partial_h = lax.dot_general(counts, sgrad, (((0,), (0,)), ((), ())), preferred_element_type=jnp.float32)
    partial_h = partial_h.reshape(regions, owned, width)
    (region_w, region_h), _ = scatter_sum(
        [partial_w, partial_h], "region", [1, 0], up, up[:1] + up[1:][::-1], joins=[0, 1],
        wires=[None, jnp.bfloat16] + [None] * (len(up) - 2),
    )
    (piece_w,), (region_h,) = scatter_sum(
        [region_w], "dom", [0], list(range(log2(doms))), riders=[region_h],
        wires=None,
    )
    weight_grad, hub_grad = gather_ordered(
        piece_w, "region", down, region_h, down[:-1][::-1] + down[-1:]
    )
    weight_grad = weight_grad.reshape(regions * span, width)
    return (activ, weight_grad, hub_grad)


def solution(mesh):
    placed = (
        P(("region", "dom"), None),
        P("region", None),
        P(("region", "dom"), None),
        P(("region", "dom")),
        P(("region", "dom"), None, None),
        P(),
        P(("region", "dom"), None),
    )
    return jax.shard_map(
        on_device,
        mesh=mesh,
        in_specs=placed,
        out_specs=(P(("region", "dom"), None), P("dom", None), P("region", None)),
        check_vma=False,
    )
```

```python
import jax
import jax.numpy as jnp
from jax import lax
from jax.sharding import PartitionSpec as P


def shifted(value, axis, steps):
    count = lax.axis_size(axis)
    initial, last = (max(0, -steps), min(count, count - steps))
    return lax.ppermute(value, axis, [(source, source + steps) for source in range(initial, last)])


def log2(n):
    bits = n.bit_length() - 1
    assert (1 << bits) == n
    return bits


def exchange(sends, axis, pairs, wire=None):
    width = sends[0].shape[-1]
    flat = jnp.concatenate([x.reshape(-1, width) for x in sends], axis=0)
    kind = flat.dtype
    flat = flat if wire is None else flat.astype(wire)
    flat = lax.ppermute(flat, axis, pairs).astype(kind)
    got, start = [], 0
    for x in sends:
        size = x.size // width
        got.append(flat[start : start + size].reshape(x.shape))
        start += size
    return got


def scatter_sum(values, axis, ats, order, other=None, riders=(), joins=None, wires=None):
    count = lax.axis_size(axis)
    levels = log2(count)
    me = lax.axis_index(axis)
    other = order if other is None else other
    joins = [0] * len(values) if joins is None else joins
    first = (me & 1) == 0
    values = [
        v.reshape(v.shape[:at] + (2,) * levels + v.shape[at + 1 :]) for v, at in zip(values, ats)
    ]
    riders = list(riders)
    held = [[[levels - 1 - k for k in range(levels)] for _ in range(2)] for _ in values]
    for step, (bit, bit_b) in enumerate(zip(order, other)):
        active = [i for i in range(len(values)) if joins[i] <= step]
        keeps, sends = [], []
        for i in active:
            v, at = values[i], ats[i]
            terms = v if isinstance(v, tuple) else (v,)
            parts = []
            for group, b in enumerate((bit, bit_b)):
                dim = at + held[i][group].index(b)
                held[i][group].remove(b)
                mine = (me >> b) & 1
                keep = sum_of([lax.dynamic_index_in_dim(t, mine, axis=dim, keepdims=False) for t in terms])
                send = sum_of([lax.dynamic_index_in_dim(t, 1 - mine, axis=dim, keepdims=False) for t in terms])
                parts.append((keep, send))
            if bit == bit_b:
                keeps.append(parts[0][0])
                sends.append(parts[0][1])
            else:
                keeps.append(jnp.where(first, parts[0][0], parts[1][0]))
                sends.append(jnp.where(first, parts[0][1], parts[1][1]))
        pairs = [(i, i ^ (1 << (bit if i & 1 == 0 else bit_b))) for i in range(count)]
        got = exchange(sends + riders, axis, pairs, None if wires is None else wires[step])
        for i, k, g in zip(active, keeps, got):
            values[i] = (k, g)
        riders = [r + g for r, g in zip(riders, got[len(keeps) :])]
    values = [sum_of(v) if isinstance(v, tuple) else v for v in values]
    return values, riders


def sum_of(terms):
    total = terms[0]
    for t in terms[1:]:
        total = total + t
    return total


def gather_ordered(value, axis, order, rider=None):
    count = lax.axis_size(axis)
    levels = log2(count)
    me = lax.axis_index(axis)
    rest = value.shape
    held = []
    for bit in order:
        pairs = [(i, i ^ (1 << bit)) for i in range(count)]
        mine = (me >> bit) & 1
        if rider is not None and bit == 0:
            keep = lax.dynamic_index_in_dim(rider, mine, axis=0, keepdims=False)
            send = lax.dynamic_index_in_dim(rider, 1 - mine, axis=0, keepdims=False)
            got, got_rider = exchange([value, send], axis, pairs)
            rider = keep + got_rider
        else:
            got = lax.ppermute(value, axis, pairs)
        low = jnp.where(mine == 0, value, got)
        high = jnp.where(mine == 0, got, value)
        value = jnp.stack([low, high], axis=len(held))
        held.append(bit)
    natural = [held.index(levels - 1 - k) for k in range(levels)]
    if natural != list(range(levels)):
        value = jnp.transpose(value, natural + list(range(levels, levels + len(rest))))
    return value.reshape((count,) + rest), rider


def layer(feats, hub_feats, hub_ids, tile_src, tile_mask, w_stack, cotangent):
    rows, width = feats.shape
    tile = tile_mask.shape[1]
    nblk = rows // tile
    per_block = tile_src.shape[0] // nblk
    hub_count = hub_ids.shape[1]
    owned = hub_feats.shape[0]
    regions = lax.axis_size("region")
    doms = lax.axis_size("dom")
    total_hubs = owned * regions
    up = list(range(log2(regions)))
    down = up[::-1]
    prev = shifted(feats[rows - tile :], "dom", 1)
    hub_table = gather_ordered(hub_feats, "region", down)[0].reshape(total_hubs, width)
    window = jnp.concatenate([prev, feats], axis=0)
    src = tile_src.reshape(nblk, per_block)
    chosen = src[:, :, None] == lax.broadcasted_iota(jnp.int32, (nblk, per_block, nblk + 1), 2)
    masks = tile_mask.reshape(nblk, per_block, tile, 1, tile)
    links = jnp.where(chosen[:, :, None, :, None], masks, 0).sum(axis=1)
    links = links.reshape(rows, (nblk + 1) * tile)
    nsum = jnp.dot(links.astype(jnp.bfloat16), window, preferred_element_type=jnp.float32)
    cnt = tile_mask.reshape(nblk, per_block, tile, tile).sum(axis=(1, 3)).reshape(rows)
    deg = 1.0 + cnt.astype(jnp.float32) + jnp.float32(hub_count)
    hub_cols = lax.broadcasted_iota(jnp.int32, (rows, total_hubs), 1)
    counts = jnp.zeros((rows, total_hubs), jnp.float32)
    for slot in range(hub_count):
        counts = counts + (hub_ids[:, slot : slot + 1] == hub_cols).astype(jnp.float32)
    counts = counts.astype(jnp.bfloat16)
    hsum = jnp.dot(counts, hub_table, preferred_element_type=jnp.float32)
    agg = ((feats.astype(jnp.float32) + nsum + hsum) / deg[:, None]).astype(jnp.bfloat16)
    inputs = jnp.concatenate([feats, agg], axis=1)
    z = jnp.dot(inputs, w_stack, preferred_element_type=jnp.float32)
    sig = jax.nn.sigmoid(z)
    activ = (z * sig).astype(jnp.bfloat16)
    dz = (cotangent.astype(jnp.float32) * sig * (1.0 + z * (1.0 - sig))).astype(jnp.bfloat16)
    partial_w = lax.dot_general(inputs, dz, (((0,), (0,)), ((), ())), preferred_element_type=jnp.float32)
    span = partial_w.shape[0] // (doms * regions)
    partial_w = partial_w.reshape(doms, regions, span, width)
    dagg = lax.dot_general(
        dz, w_stack[width:], (((1,), (1,)), ((), ())), preferred_element_type=jnp.float32
    )
    sgrad = (dagg / deg[:, None]).astype(jnp.bfloat16)
    partial_h = lax.dot_general(counts, sgrad, (((0,), (0,)), ((), ())), preferred_element_type=jnp.float32)
    partial_h = partial_h.reshape(regions, owned, width)
    (region_w, region_h), _ = scatter_sum(
        [partial_w, partial_h], "region", [1, 0], up, up[:1] + up[1:][::-1], joins=[0, 1],
        wires=[None, jnp.bfloat16] + [None] * (len(up) - 2),
    )
    (piece_w,), (region_h,) = scatter_sum(
        [region_w], "dom", [0], list(range(log2(doms))), riders=[region_h],
        wires=None,
    )
    weight_grad, hub_grad = gather_ordered(piece_w, "region", down, region_h)
    weight_grad = weight_grad.reshape(regions * span, width)
    return (activ, weight_grad, hub_grad)


def solution(mesh):
    placed = (
        P(("region", "dom"), None),
        P("region", None),
        P(("region", "dom"), None),
        P(("region", "dom")),
        P(("region", "dom"), None, None),
        P(),
        P(("region", "dom"), None),
    )
    return jax.shard_map(
        layer,
        mesh=mesh,
        in_specs=placed,
        out_specs=(P(("region", "dom"), None), P("dom", None), P("region", None)),
        check_vma=False,
    )
```

```python
import jax
import jax.numpy as jnp
from jax import lax
from jax.sharding import PartitionSpec as P


def shifted(value, axis, steps):
    count = lax.axis_size(axis)
    initial, last = (max(0, -steps), min(count, count - steps))
    return lax.ppermute(value, axis, [(source, source + steps) for source in range(initial, last)])


def log2(n):
    bits = n.bit_length() - 1
    assert (1 << bits) == n
    return bits


def exchange(sends, axis, pairs, wire=None):
    width = sends[0].shape[-1]
    flat = jnp.concatenate([x.reshape(-1, width) for x in sends], axis=0)
    kind = flat.dtype
    flat = flat if wire is None else flat.astype(wire)
    flat = lax.ppermute(flat, axis, pairs).astype(kind)
    got, start = [], 0
    for x in sends:
        size = x.size // width
        got.append(flat[start : start + size].reshape(x.shape))
        start += size
    return got


def scatter_sum(values, axis, ats, order, other=None, riders=(), joins=None, wires=None):
    count = lax.axis_size(axis)
    levels = log2(count)
    me = lax.axis_index(axis)
    other = order if other is None else other
    joins = [0] * len(values) if joins is None else joins
    first = (me & 1) == 0
    values = [
        v.reshape(v.shape[:at] + (2,) * levels + v.shape[at + 1 :]) for v, at in zip(values, ats)
    ]
    riders = list(riders)
    held = [[[levels - 1 - k for k in range(levels)] for _ in range(2)] for _ in values]
    for step, (bit, bit_b) in enumerate(zip(order, other)):
        active = [i for i in range(len(values)) if joins[i] <= step]
        keeps, sends = [], []
        for i in active:
            v, at = values[i], ats[i]
            parts = []
            for group, b in enumerate((bit, bit_b)):
                dim = at + held[i][group].index(b)
                held[i][group].remove(b)
                mine = (me >> b) & 1
                keep = lax.dynamic_index_in_dim(v, mine, axis=dim, keepdims=False)
                send = lax.dynamic_index_in_dim(v, 1 - mine, axis=dim, keepdims=False)
                parts.append((keep, send))
            if bit == bit_b:
                keeps.append(parts[0][0])
                sends.append(parts[0][1])
            else:
                keeps.append(jnp.where(first, parts[0][0], parts[1][0]))
                sends.append(jnp.where(first, parts[0][1], parts[1][1]))
        pairs = [(i, i ^ (1 << (bit if i & 1 == 0 else bit_b))) for i in range(count)]
        got = exchange(sends + riders, axis, pairs, None if wires is None else wires[step])
        for i, k, g in zip(active, keeps, got):
            values[i] = k + g
        riders = [r + g for r, g in zip(riders, got[len(keeps) :])]
    return values, riders


def gather_ordered(value, axis, order, rider=None):
    count = lax.axis_size(axis)
    levels = log2(count)
    me = lax.axis_index(axis)
    rest = value.shape
    held = []
    for bit in order:
        pairs = [(i, i ^ (1 << bit)) for i in range(count)]
        mine = (me >> bit) & 1
        if rider is not None and bit == 0:
            keep = lax.dynamic_index_in_dim(rider, mine, axis=0, keepdims=False)
            send = lax.dynamic_index_in_dim(rider, 1 - mine, axis=0, keepdims=False)
            got, got_rider = exchange([value, send], axis, pairs)
            rider = keep + got_rider
        else:
            got = lax.ppermute(value, axis, pairs)
        low = jnp.where(mine == 0, value, got)
        high = jnp.where(mine == 0, got, value)
        value = jnp.stack([low, high], axis=len(held))
        held.append(bit)
    natural = [held.index(levels - 1 - k) for k in range(levels)]
    if natural != list(range(levels)):
        value = jnp.transpose(value, natural + list(range(levels, levels + len(rest))))
    return value.reshape((count,) + rest), rider


def layer(feats, hub_feats, hub_ids, tile_src, tile_mask, w_stack, cotangent):
    rows, width = feats.shape
    tile = tile_mask.shape[1]
    nblk = rows // tile
    per_block = tile_src.shape[0] // nblk
    hub_count = hub_ids.shape[1]
    owned = hub_feats.shape[0]
    regions = lax.axis_size("region")
    doms = lax.axis_size("dom")
    total_hubs = owned * regions
    up = list(range(log2(regions)))
    down = up[::-1]
    prev = shifted(feats[rows - tile :], "dom", 1)
    hub_table = gather_ordered(hub_feats, "region", down)[0].reshape(total_hubs, width)
    window = jnp.concatenate([prev, feats], axis=0)
    src = tile_src.reshape(nblk, per_block)
    chosen = src[:, :, None] == lax.broadcasted_iota(jnp.int32, (nblk, per_block, nblk + 1), 2)
    masks = tile_mask.reshape(nblk, per_block, tile, 1, tile)
    links = jnp.where(chosen[:, :, None, :, None], masks, 0).sum(axis=1)
    links = links.reshape(rows, (nblk + 1) * tile)
    nsum = jnp.dot(links.astype(jnp.bfloat16), window, preferred_element_type=jnp.float32)
    cnt = tile_mask.reshape(nblk, per_block, tile, tile).sum(axis=(1, 3)).reshape(rows)
    deg = 1.0 + cnt.astype(jnp.float32) + jnp.float32(hub_count)
    hub_cols = lax.broadcasted_iota(jnp.int32, (rows, total_hubs), 1)
    counts = jnp.zeros((rows, total_hubs), jnp.float32)
    for slot in range(hub_count):
        counts = counts + (hub_ids[:, slot : slot + 1] == hub_cols).astype(jnp.float32)
    counts = counts.astype(jnp.bfloat16)
    hsum = jnp.dot(counts, hub_table, preferred_element_type=jnp.float32)
    agg = ((feats.astype(jnp.float32) + nsum + hsum) / deg[:, None]).astype(jnp.bfloat16)
    inputs = jnp.concatenate([feats, agg], axis=1)
    z_self = jnp.dot(feats, w_stack[:width], preferred_element_type=jnp.float32)
    z = z_self + jnp.dot(agg, w_stack[width:], preferred_element_type=jnp.float32)
    sig = jax.nn.sigmoid(z)
    activ = (z * sig).astype(jnp.bfloat16)
    dz = (cotangent.astype(jnp.float32) * sig * (1.0 + z * (1.0 - sig))).astype(jnp.bfloat16)
    partial_w = lax.dot_general(inputs, dz, (((0,), (0,)), ((), ())), preferred_element_type=jnp.float32)
    span = partial_w.shape[0] // (doms * regions)
    partial_w = partial_w.reshape(doms, regions, span, width)
    dagg = lax.dot_general(
        dz, w_stack[width:], (((1,), (1,)), ((), ())), preferred_element_type=jnp.float32
    )
    sgrad = (dagg / deg[:, None]).astype(jnp.bfloat16)
    partial_h = lax.dot_general(counts, sgrad, (((0,), (0,)), ((), ())), preferred_element_type=jnp.float32)
    partial_h = partial_h.reshape(regions, owned, width)
    (region_w, region_h), _ = scatter_sum(
        [partial_w, partial_h], "region", [1, 0], up, up[:1] + up[1:][::-1], joins=[0, 1],
        wires=[None] + [jnp.bfloat16] * (len(up) - 1),
    )
    (piece_w,), (region_h,) = scatter_sum(
        [region_w], "dom", [0], list(range(log2(doms))), riders=[region_h],
        wires=None,
    )
    weight_grad, hub_grad = gather_ordered(piece_w, "region", down, region_h)
    weight_grad = weight_grad.reshape(regions * span, width)
    return (activ, weight_grad, hub_grad)


def solution(mesh):
    placed = (
        P(("region", "dom"), None),
        P("region", None),
        P(("region", "dom"), None),
        P(("region", "dom")),
        P(("region", "dom"), None, None),
        P(),
        P(("region", "dom"), None),
    )
    return jax.shard_map(
        layer,
        mesh=mesh,
        in_specs=placed,
        out_specs=(P(("region", "dom"), None), P("dom", None), P("region", None)),
        check_vma=False,
    )
```

```python
import jax
import jax.numpy as jnp
from jax import lax
from jax.sharding import PartitionSpec as P


def shifted(value, axis, steps):
    count = lax.axis_size(axis)
    initial, last = (max(0, -steps), min(count, count - steps))
    return lax.ppermute(value, axis, [(source, source + steps) for source in range(initial, last)])


def log2(n):
    bits = n.bit_length() - 1
    assert (1 << bits) == n
    return bits


def exchange(sends, axis, pairs, wire=None):
    width = sends[0].shape[-1]
    flat = jnp.concatenate([x.reshape(-1, width) for x in sends], axis=0)
    kind = flat.dtype
    flat = flat if wire is None else flat.astype(wire)
    flat = lax.ppermute(flat, axis, pairs).astype(kind)
    got, start = [], 0
    for x in sends:
        size = x.size // width
        got.append(flat[start : start + size].reshape(x.shape))
        start += size
    return got


def scatter_sum(values, axis, ats, order, other=None, riders=(), joins=None, wires=None):
    count = lax.axis_size(axis)
    levels = log2(count)
    me = lax.axis_index(axis)
    other = order if other is None else other
    joins = [0] * len(values) if joins is None else joins
    first = (me & 1) == 0
    values = [
        v.reshape(v.shape[:at] + (2,) * levels + v.shape[at + 1 :]) for v, at in zip(values, ats)
    ]
    riders = list(riders)
    held = [[[levels - 1 - k for k in range(levels)] for _ in range(2)] for _ in values]
    for step, (bit, bit_b) in enumerate(zip(order, other)):
        active = [i for i in range(len(values)) if joins[i] <= step]
        keeps, sends = [], []
        for i in active:
            v, at = values[i], ats[i]
            parts = []
            for group, b in enumerate((bit, bit_b)):
                dim = at + held[i][group].index(b)
                held[i][group].remove(b)
                mine = (me >> b) & 1
                keep = lax.dynamic_index_in_dim(v, mine, axis=dim, keepdims=False)
                send = lax.dynamic_index_in_dim(v, 1 - mine, axis=dim, keepdims=False)
                parts.append((keep, send))
            if bit == bit_b:
                keeps.append(parts[0][0])
                sends.append(parts[0][1])
            else:
                keeps.append(jnp.where(first, parts[0][0], parts[1][0]))
                sends.append(jnp.where(first, parts[0][1], parts[1][1]))
        pairs = [(i, i ^ (1 << (bit if i & 1 == 0 else bit_b))) for i in range(count)]
        got = exchange(sends + riders, axis, pairs, None if wires is None else wires[step])
        for i, k, g in zip(active, keeps, got):
            values[i] = k + g
        riders = [r + g for r, g in zip(riders, got[len(keeps) :])]
    return values, riders


def gather_ordered(value, axis, order, rider=None):
    count = lax.axis_size(axis)
    levels = log2(count)
    me = lax.axis_index(axis)
    rest = value.shape
    held = []
    for bit in order:
        pairs = [(i, i ^ (1 << bit)) for i in range(count)]
        mine = (me >> bit) & 1
        if rider is not None and bit == 0:
            keep = lax.dynamic_index_in_dim(rider, mine, axis=0, keepdims=False)
            send = lax.dynamic_index_in_dim(rider, 1 - mine, axis=0, keepdims=False)
            got, got_rider = exchange([value, send], axis, pairs)
            rider = keep + got_rider
        else:
            got = lax.ppermute(value, axis, pairs)
        low = jnp.where(mine == 0, value, got)
        high = jnp.where(mine == 0, got, value)
        value = jnp.stack([low, high], axis=len(held))
        held.append(bit)
    natural = [held.index(levels - 1 - k) for k in range(levels)]
    if natural != list(range(levels)):
        value = jnp.transpose(value, natural + list(range(levels, levels + len(rest))))
    return value.reshape((count,) + rest), rider


def gather_small(value, axis):
    count = lax.axis_size(axis)
    spread = jnp.broadcast_to(value[None], (count,) + value.shape)
    return lax.all_to_all(spread, axis, 0, 0)


def layer(feats, hub_feats, hub_ids, tile_src, tile_mask, w_stack, cotangent):
    rows, width = feats.shape
    tile = tile_mask.shape[1]
    nblk = rows // tile
    per_block = tile_src.shape[0] // nblk
    hub_count = hub_ids.shape[1]
    owned = hub_feats.shape[0]
    regions = lax.axis_size("region")
    doms = lax.axis_size("dom")
    total_hubs = owned * regions
    up = list(range(log2(regions)))
    down = up[::-1]
    prev = shifted(feats[rows - tile :], "dom", 1)
    hub_table = gather_small(hub_feats, "region").reshape(total_hubs, width)
    window = jnp.concatenate([prev, feats], axis=0)
    src = tile_src.reshape(nblk, per_block)
    chosen = src[:, :, None] == lax.broadcasted_iota(jnp.int32, (nblk, per_block, nblk + 1), 2)
    masks = tile_mask.reshape(nblk, per_block, tile, 1, tile)
    links = jnp.where(chosen[:, :, None, :, None], masks, 0).sum(axis=1)
    links = links.reshape(rows, (nblk + 1) * tile)
    cnt = links.sum(axis=1)
    nsum = jnp.dot(links.astype(jnp.bfloat16), window, preferred_element_type=jnp.float32)
    deg = 1.0 + cnt.astype(jnp.float32) + jnp.float32(hub_count)
    hub_cols = lax.broadcasted_iota(jnp.int32, (rows, total_hubs), 1)
    counts = jnp.zeros((rows, total_hubs), jnp.float32)
    for slot in range(hub_count):
        counts = counts + (hub_ids[:, slot : slot + 1] == hub_cols).astype(jnp.float32)
    counts = counts.astype(jnp.bfloat16)
    hsum = jnp.dot(counts, hub_table, preferred_element_type=jnp.float32)
    agg = ((feats.astype(jnp.float32) + nsum + hsum) / deg[:, None]).astype(jnp.bfloat16)
    inputs = jnp.concatenate([feats, agg], axis=1)
    z = jnp.dot(inputs, w_stack, preferred_element_type=jnp.float32)
    sig = jax.nn.sigmoid(z)
    activ = (z * sig).astype(jnp.bfloat16)
    dz = (cotangent.astype(jnp.float32) * sig * (1.0 + z * (1.0 - sig))).astype(jnp.bfloat16)
    partial_w = lax.dot_general(inputs, dz, (((0,), (0,)), ((), ())), preferred_element_type=jnp.float32)
    span = partial_w.shape[0] // (doms * regions)
    partial_w = partial_w.reshape(doms, regions, span, width)
    dagg = lax.dot_general(
        dz, w_stack[width:], (((1,), (1,)), ((), ())), preferred_element_type=jnp.float32
    )
    sgrad = (dagg / deg[:, None]).astype(jnp.bfloat16)
    partial_h = lax.dot_general(counts, sgrad, (((0,), (0,)), ((), ())), preferred_element_type=jnp.float32)
    partial_h = partial_h.reshape(regions, owned, width)
    (region_w, region_h), _ = scatter_sum(
        [partial_w, partial_h], "region", [1, 0], up, up[:1] + up[1:][::-1], joins=[0, 1],
        wires=[None] + [jnp.bfloat16] * (len(up) - 1),
    )
    (piece_w,), (region_h,) = scatter_sum(
        [region_w], "dom", [0], list(range(log2(doms))), riders=[region_h],
        wires=None,
    )
    weight_grad, hub_grad = gather_ordered(piece_w, "region", down, region_h)
    weight_grad = weight_grad.reshape(regions * span, width)
    return (activ, weight_grad, hub_grad)


def solution(mesh):
    placed = (
        P(("region", "dom"), None),
        P("region", None),
        P(("region", "dom"), None),
        P(("region", "dom")),
        P(("region", "dom"), None, None),
        P(),
        P(("region", "dom"), None),
    )
    return jax.shard_map(
        layer,
        mesh=mesh,
        in_specs=placed,
        out_specs=(P(("region", "dom"), None), P("dom", None), P("region", None)),
        check_vma=False,
    )
```

```python
import jax
import jax.numpy as jnp
from jax import lax
from jax.sharding import PartitionSpec as P


def shifted(value, axis, steps):
    count = lax.axis_size(axis)
    initial, last = (max(0, -steps), min(count, count - steps))
    return lax.ppermute(value, axis, [(source, source + steps) for source in range(initial, last)])


def log2(n):
    bits = n.bit_length() - 1
    assert (1 << bits) == n
    return bits


def exchange(sends, axis, pairs, wire=None):
    width = sends[0].shape[-1]
    flat = jnp.concatenate([x.reshape(-1, width) for x in sends], axis=0)
    kind = flat.dtype
    flat = flat if wire is None else flat.astype(wire)
    flat = lax.ppermute(flat, axis, pairs).astype(kind)
    got, start = [], 0
    for x in sends:
        size = x.size // width
        got.append(flat[start : start + size].reshape(x.shape))
        start += size
    return got


def scatter_sum(values, axis, ats, order, other=None, riders=(), joins=None, wires=None):
    count = lax.axis_size(axis)
    levels = log2(count)
    me = lax.axis_index(axis)
    other = order if other is None else other
    joins = [0] * len(values) if joins is None else joins
    first = (me & 1) == 0
    values = [
        v.reshape(v.shape[:at] + (2,) * levels + v.shape[at + 1 :]) for v, at in zip(values, ats)
    ]
    riders = list(riders)
    held = [[[levels - 1 - k for k in range(levels)] for _ in range(2)] for _ in values]
    for step, (bit, bit_b) in enumerate(zip(order, other)):
        active = [i for i in range(len(values)) if joins[i] <= step]
        keeps, sends = [], []
        for i in active:
            v, at = values[i], ats[i]
            parts = []
            for group, b in enumerate((bit, bit_b)):
                dim = at + held[i][group].index(b)
                held[i][group].remove(b)
                mine = (me >> b) & 1
                keep = lax.dynamic_index_in_dim(v, mine, axis=dim, keepdims=False)
                send = lax.dynamic_index_in_dim(v, 1 - mine, axis=dim, keepdims=False)
                parts.append((keep, send))
            if bit == bit_b:
                keeps.append(parts[0][0])
                sends.append(parts[0][1])
            else:
                keeps.append(jnp.where(first, parts[0][0], parts[1][0]))
                sends.append(jnp.where(first, parts[0][1], parts[1][1]))
        pairs = [(i, i ^ (1 << (bit if i & 1 == 0 else bit_b))) for i in range(count)]
        got = exchange(sends + riders, axis, pairs, None if wires is None else wires[step])
        for i, k, g in zip(active, keeps, got):
            values[i] = k + g
        riders = [r + g for r, g in zip(riders, got[len(keeps) :])]
    return values, riders


def gather_ordered(value, axis, order, rider=None):
    count = lax.axis_size(axis)
    levels = log2(count)
    me = lax.axis_index(axis)
    rest = value.shape
    held = []
    for bit in order:
        pairs = [(i, i ^ (1 << bit)) for i in range(count)]
        mine = (me >> bit) & 1
        if rider is not None and bit == 0:
            keep = lax.dynamic_index_in_dim(rider, mine, axis=0, keepdims=False)
            send = lax.dynamic_index_in_dim(rider, 1 - mine, axis=0, keepdims=False)
            got, got_rider = exchange([value, send], axis, pairs)
            rider = keep + got_rider
        else:
            got = lax.ppermute(value, axis, pairs)
        low = jnp.where(mine == 0, value, got)
        high = jnp.where(mine == 0, got, value)
        value = jnp.stack([low, high], axis=len(held))
        held.append(bit)
    natural = [held.index(levels - 1 - k) for k in range(levels)]
    if natural != list(range(levels)):
        value = jnp.transpose(value, natural + list(range(levels, levels + len(rest))))
    return value.reshape((count,) + rest), rider


def layer(feats, hub_feats, hub_ids, tile_src, tile_mask, w_stack, cotangent):
    rows, width = feats.shape
    tile = tile_mask.shape[1]
    nblk = rows // tile
    per_block = tile_src.shape[0] // nblk
    hub_count = hub_ids.shape[1]
    owned = hub_feats.shape[0]
    regions = lax.axis_size("region")
    doms = lax.axis_size("dom")
    total_hubs = owned * regions
    up = list(range(log2(regions)))
    down = up[::-1]
    prev = shifted(feats, "dom", 1)[rows - tile :]
    hub_table = gather_ordered(hub_feats, "region", down)[0].reshape(total_hubs, width)
    window = jnp.concatenate([prev, feats], axis=0)
    src = tile_src.reshape(nblk, per_block)
    chosen = src[:, :, None] == lax.broadcasted_iota(jnp.int32, (nblk, per_block, nblk + 1), 2)
    masks = tile_mask.reshape(nblk, per_block, tile, 1, tile)
    links = jnp.where(chosen[:, :, None, :, None], masks, 0).sum(axis=1)
    links = links.reshape(rows, (nblk + 1) * tile)
    nsum = jnp.dot(links.astype(jnp.bfloat16), window, preferred_element_type=jnp.float32)
    cnt = tile_mask.reshape(nblk, per_block, tile, tile).sum(axis=(1, 3)).reshape(rows)
    deg = 1.0 + cnt.astype(jnp.float32) + jnp.float32(hub_count)
    hub_cols = lax.broadcasted_iota(jnp.int32, (rows, total_hubs), 1)
    counts = jnp.zeros((rows, total_hubs), jnp.float32)
    for slot in range(hub_count):
        counts = counts + (hub_ids[:, slot : slot + 1] == hub_cols).astype(jnp.float32)
    counts = counts.astype(jnp.bfloat16)
    hsum = jnp.dot(counts, hub_table, preferred_element_type=jnp.float32)
    agg = ((feats.astype(jnp.float32) + nsum + hsum) / deg[:, None]).astype(jnp.bfloat16)
    inputs = jnp.concatenate([feats, agg], axis=1)
    z = jnp.dot(inputs, w_stack, preferred_element_type=jnp.float32)
    sig = jax.nn.sigmoid(z)
    activ = (z * sig).astype(jnp.bfloat16)
    dz = (cotangent.astype(jnp.float32) * sig * (1.0 + z * (1.0 - sig))).astype(jnp.bfloat16)
    partial_w = lax.dot_general(inputs, dz, (((0,), (0,)), ((), ())), preferred_element_type=jnp.float32)
    span = partial_w.shape[0] // (doms * regions)
    partial_w = partial_w.reshape(doms, regions, span, width)
    dagg = lax.dot_general(
        dz, w_stack[width:], (((1,), (1,)), ((), ())), preferred_element_type=jnp.float32
    )
    sgrad = (dagg / deg[:, None]).astype(jnp.bfloat16)
    partial_h = lax.dot_general(counts, sgrad, (((0,), (0,)), ((), ())), preferred_element_type=jnp.float32)
    partial_h = partial_h.reshape(regions, owned, width)
    (region_w, region_h), _ = scatter_sum(
        [partial_w, partial_h], "region", [1, 0], up, up[:1] + up[1:][::-1], joins=[0, 1],
        wires=[None] + [jnp.bfloat16] * (len(up) - 1),
    )
    (piece_w,), (region_h,) = scatter_sum(
        [region_w], "dom", [0], list(range(log2(doms))), riders=[region_h],
        wires=None,
    )
    weight_grad, hub_grad = gather_ordered(piece_w, "region", down, region_h)
    weight_grad = weight_grad.reshape(regions * span, width)
    return (activ, weight_grad, hub_grad)


def solution(mesh):
    placed = (
        P(("region", "dom"), None),
        P("region", None),
        P(("region", "dom"), None),
        P(("region", "dom")),
        P(("region", "dom"), None, None),
        P(),
        P(("region", "dom"), None),
    )
    return jax.shard_map(
        layer,
        mesh=mesh,
        in_specs=placed,
        out_specs=(P(("region", "dom"), None), P("dom", None), P("region", None)),
        check_vma=False,
    )
```

```python
import jax
import jax.numpy as jnp
from jax import lax
from jax.sharding import PartitionSpec as P


def shifted(value, axis, steps):
    count = lax.axis_size(axis)
    initial, last = (max(0, -steps), min(count, count - steps))
    return lax.ppermute(value, axis, [(source, source + steps) for source in range(initial, last)])


def log2(n):
    bits = n.bit_length() - 1
    assert (1 << bits) == n
    return bits


def exchange(sends, axis, pairs, wire=None):
    width = sends[0].shape[-1]
    flat = jnp.concatenate([x.reshape(-1, width) for x in sends], axis=0)
    kind = flat.dtype
    flat = flat if wire is None else flat.astype(wire)
    flat = lax.ppermute(flat, axis, pairs).astype(kind)
    got, start = [], 0
    for x in sends:
        size = x.size // width
        got.append(flat[start : start + size].reshape(x.shape))
        start += size
    return got


def scatter_sum(values, axis, ats, order, other=None, riders=(), joins=None, wires=None):
    count = lax.axis_size(axis)
    levels = log2(count)
    me = lax.axis_index(axis)
    other = order if other is None else other
    joins = [0] * len(values) if joins is None else joins
    first = (me & 1) == 0
    values = [
        v.reshape(v.shape[:at] + (2,) * levels + v.shape[at + 1 :]) for v, at in zip(values, ats)
    ]
    riders = list(riders)
    held = [[[levels - 1 - k for k in range(levels)] for _ in range(2)] for _ in values]
    for step, (bit, bit_b) in enumerate(zip(order, other)):
        active = [i for i in range(len(values)) if joins[i] <= step]
        keeps, sends = [], []
        for i in active:
            v, at = values[i], ats[i]
            parts = []
            for group, b in enumerate((bit, bit_b)):
                dim = at + held[i][group].index(b)
                held[i][group].remove(b)
                mine = (me >> b) & 1
                keep = lax.dynamic_index_in_dim(v, mine, axis=dim, keepdims=False)
                send = lax.dynamic_index_in_dim(v, 1 - mine, axis=dim, keepdims=False)
                parts.append((keep, send))
            if bit == bit_b:
                keeps.append(parts[0][0])
                sends.append(parts[0][1])
            else:
                keeps.append(jnp.where(first, parts[0][0], parts[1][0]))
                sends.append(jnp.where(first, parts[0][1], parts[1][1]))
        pairs = [(i, i ^ (1 << (bit if i & 1 == 0 else bit_b))) for i in range(count)]
        got = exchange(sends + riders, axis, pairs, None if wires is None else wires[step])
        for i, k, g in zip(active, keeps, got):
            values[i] = k + g
        riders = [r + g for r, g in zip(riders, got[len(keeps) :])]
    return values, riders


def gather_ordered(value, axis, order, rider=None):
    count = lax.axis_size(axis)
    levels = log2(count)
    me = lax.axis_index(axis)
    rest = value.shape
    held = []
    for bit in order:
        pairs = [(i, i ^ (1 << bit)) for i in range(count)]
        mine = (me >> bit) & 1
        if rider is not None and bit == 0:
            keep = lax.dynamic_index_in_dim(rider, mine, axis=0, keepdims=False)
            send = lax.dynamic_index_in_dim(rider, 1 - mine, axis=0, keepdims=False)
            got, got_rider = exchange([value, send], axis, pairs)
            rider = keep + got_rider
        else:
            got = lax.ppermute(value, axis, pairs)
        value = jnp.stack([value, value], axis=len(held))
        value = lax.dynamic_update_index_in_dim(value, got, 1 - mine, axis=len(held))
        held.append(bit)
    natural = [held.index(levels - 1 - k) for k in range(levels)]
    if natural != list(range(levels)):
        value = jnp.transpose(value, natural + list(range(levels, levels + len(rest))))
    return value.reshape((count,) + rest), rider


def layer(feats, hub_feats, hub_ids, tile_src, tile_mask, w_stack, cotangent):
    rows, width = feats.shape
    tile = tile_mask.shape[1]
    nblk = rows // tile
    per_block = tile_src.shape[0] // nblk
    hub_count = hub_ids.shape[1]
    owned = hub_feats.shape[0]
    regions = lax.axis_size("region")
    doms = lax.axis_size("dom")
    total_hubs = owned * regions
    up = list(range(log2(regions)))
    down = up[::-1]
    prev = shifted(feats[rows - tile :], "dom", 1)
    hub_table = gather_ordered(hub_feats, "region", down)[0].reshape(total_hubs, width)
    window = jnp.concatenate([prev, feats], axis=0)
    src = tile_src.reshape(nblk, per_block)
    chosen = src[:, :, None] == lax.broadcasted_iota(jnp.int32, (nblk, per_block, nblk + 1), 2)
    masks = tile_mask.reshape(nblk, per_block, tile, 1, tile)
    links = jnp.where(chosen[:, :, None, :, None], masks, 0).sum(axis=1)
    links = links.reshape(rows, (nblk + 1) * tile)
    nsum = jnp.dot(links.astype(jnp.bfloat16), window, preferred_element_type=jnp.float32)
    cnt = tile_mask.reshape(nblk, per_block, tile, tile).sum(axis=(1, 3)).reshape(rows)
    deg = 1.0 + cnt.astype(jnp.float32) + jnp.float32(hub_count)
    hub_cols = lax.broadcasted_iota(jnp.int32, (rows, total_hubs), 1)
    counts = jnp.zeros((rows, total_hubs), jnp.float32)
    for slot in range(hub_count):
        counts = counts + (hub_ids[:, slot : slot + 1] == hub_cols).astype(jnp.float32)
    counts = counts.astype(jnp.bfloat16)
    hsum = jnp.dot(counts, hub_table, preferred_element_type=jnp.float32)
    agg = ((feats.astype(jnp.float32) + nsum + hsum) / deg[:, None]).astype(jnp.bfloat16)
    inputs = jnp.concatenate([feats, agg], axis=1)
    z = jnp.dot(inputs, w_stack, preferred_element_type=jnp.float32)
    sig = jax.nn.sigmoid(z)
    activ = (z * sig).astype(jnp.bfloat16)
    dz = (cotangent.astype(jnp.float32) * sig * (1.0 + z * (1.0 - sig))).astype(jnp.bfloat16)
    partial_w = lax.dot_general(inputs, dz, (((0,), (0,)), ((), ())), preferred_element_type=jnp.float32)
    span = partial_w.shape[0] // (doms * regions)
    partial_w = partial_w.reshape(doms, regions, span, width)
    dagg = lax.dot_general(
        dz, w_stack[width:], (((1,), (1,)), ((), ())), preferred_element_type=jnp.float32
    )
    sgrad = (dagg / deg[:, None]).astype(jnp.bfloat16)
    partial_h = lax.dot_general(counts, sgrad, (((0,), (0,)), ((), ())), preferred_element_type=jnp.float32)
    partial_h = partial_h.reshape(regions, owned, width)
    (region_w, region_h), _ = scatter_sum(
        [partial_w, partial_h], "region", [1, 0], up, up[:1] + up[1:][::-1], joins=[0, 1],
        wires=[None] + [jnp.bfloat16] * (len(up) - 1),
    )
    (piece_w,), (region_h,) = scatter_sum(
        [region_w], "dom", [0], list(range(log2(doms))), riders=[region_h],
        wires=None,
    )
    weight_grad, hub_grad = gather_ordered(piece_w, "region", down, region_h)
    weight_grad = weight_grad.reshape(regions * span, width)
    return (activ, weight_grad, hub_grad)


def solution(mesh):
    placed = (
        P(("region", "dom"), None),
        P("region", None),
        P(("region", "dom"), None),
        P(("region", "dom")),
        P(("region", "dom"), None, None),
        P(),
        P(("region", "dom"), None),
    )
    return jax.shard_map(
        layer,
        mesh=mesh,
        in_specs=placed,
        out_specs=(P(("region", "dom"), None), P("dom", None), P("region", None)),
        check_vma=False,
    )
```
